256 devices in a mesh: tm: 8 (over x, core), sx: 8 (over z), sy: 4 (over y).
Axes of the slice: x: 4, y: 4, z: 8, core: 2. Of those that a mesh axis runs over, the one named last changes fastest.
Arguments:
- initial_saturation: float32 [32, 64, 256], P('sx', 'sy'), may hold values from 0.05 to 0.95
- permeability: float32 [32, 64, 256], P('sx', 'sy'), may hold values from 0.1 to 10
- porosity: float32 [32, 64, 256], P('sx', 'sy'), may hold values from 0.1 to 0.3
- source_rate: float32 [32, 64, 256], P('sx', 'sy'), may hold values from -3 to 3
- rock_type: int32 [16, 32, 128], P('sx', 'sy'), may hold values from 0 to 3
- water_endpoint: float32 [4], replicated, may hold values from 0.3 to 1
- oil_endpoint: float32 [4], replicated, may hold values from 0.3 to 1
Outputs:
- end_saturation: float32 [8, 32, 64, 256], P('tm', 'sx', 'sy')
- last_pressure: float32 [8, 32, 64, 256], P('tm', 'sx', 'sy')
The draws below stay inside these ranges and needn't reach their ends.
All inputs are finite; a program needn't handle non-finite values.
Results may differ from the reference program's by a relative error of at most 0.0003.
Values sent between devices are 32-bit elements; how exact they have to be, the bound alone decides.
No kernel may reach another device: no remote copies, remote signals or barrier semaphores. Data moves between devices by JAX's collectives and lax.ppermute only.
A program may use at most 64 MiB of HBM per device.

```python
import math
import jax
import jax.numpy as jnp

CZ = 256
FSTEPS = 1
NEWTON = 2
CG_ITERS = 3
SWEEPS = 3
PARAREAL = 2
ROCKS = 4
SLICES = 8
NX = 32
NY = 64


def plant(entries, key, smallest, high):
    longest = entries.shape.index(max(entries.shape))
    spots = []
    for shift in (0, 1):
        where = [jax.random.randint(jax.random.fold_in(key, axis), (), 0, length) for axis, length in enumerate(entries.shape)]
        where[longest] = (where[longest] + shift) % entries.shape[longest]
        spots.append(tuple(where))
    return entries.at[spots[0]].set(smallest).at[spots[1]].set(high)


def steps_of(stream_key, extent, split, least, largest):
    level, own = 1.0, jax.random.fold_in(stream_key, 6)
    for position, blocks in split:
        draws = jnp.exp(jax.random.uniform(jax.random.fold_in(own, position), (blocks,), jnp.float32, least / len(split), largest / len(split)))
        level = level * jnp.repeat(draws, extent[position] // blocks).reshape([-1 if axis == position else 1 for axis in range(len(extent))])
    return level


def noise(key, shape, width, limit, split=(), kind=jnp.bfloat16):
    array = jax.random.normal(key, shape, jnp.float32) * width
    if len(split) > 0:
        array = steps_of(key, shape, split, -0.22, 0.18) * array
    return jnp.clip(array, min=-limit, max=limit).astype(kind)


def setup_inputs(seed: int = 0) -> dict:
    splits = jax.random.split(jax.random.key(seed), 8)
    initial_saturation = jnp.clip(0.05 + 0.9 * jax.random.uniform(splits[0], (NX, NY, CZ), jnp.float32) ** steps_of(splits[0], (NX, NY, CZ), ((0, 8), (1, 4)), -0.2, 0.2), 0.05, 0.95)
    permeability = jnp.clip(jnp.exp(math.log(10.0) - 4.6051702 * jax.random.uniform(splits[1], (NX, NY, CZ), jnp.float32) ** steps_of(splits[1], (NX, NY, CZ), ((0, 8), (1, 4)), -0.2, 0.2)), 0.1, 10.0)
    porosity = jnp.clip(0.1 + 0.20000001043081284 * jax.random.uniform(splits[2], (NX, NY, CZ), jnp.float32) ** steps_of(splits[2], (NX, NY, CZ), ((0, 8), (1, 4)), -0.2, 0.2), 0.1, 0.3)
    source_rate = noise(splits[3], (NX, NY, CZ), 0.5, 3.0, ((0, 8), (1, 4)), jnp.float32)
    rock_type = plant(jax.random.randint(splits[4], (NX // 2, NY // 2, CZ // 2), 0, ROCKS), jax.random.fold_in(splits[4], 1), 0, ROCKS - 1).astype(jnp.int32)
    water_endpoint = jnp.clip(jnp.exp(jax.random.uniform(splits[5], (ROCKS,), jnp.float32, math.log(0.3), math.log(1.0))), 0.3, 1.0)
    oil_endpoint = jnp.clip(jnp.exp(jax.random.uniform(splits[6], (ROCKS,), jnp.float32, math.log(0.3), math.log(1.0))), 0.3, 1.0)
    return {"initial_saturation": initial_saturation, "permeability": permeability, "porosity": porosity, "source_rate": source_rate, "rock_type": rock_type, "water_endpoint": water_endpoint, "oil_endpoint": oil_endpoint}


mu_water = 1.0
mu_oil = 4.0
compress = 0.05
step_dt = 0.25
damping = 0.8


def lookup(rock_cells, end_values):
    summed_total = jnp.zeros(rock_cells.shape, end_values.dtype)
    for rock_kind in range(ROCKS):
        summed_total = summed_total + jnp.where(rock_cells == rock_kind, end_values[rock_kind], jnp.zeros((), end_values.dtype))
    return summed_total


def restrict(volume):
    return volume.reshape(volume.shape[0] // 2, 2, volume.shape[1] // 2, 2, volume.shape[2] // 2, 2).mean(axis=(1, 3, 5))


def prolong(volume):
    first, second, third = volume.shape
    spread_out = jnp.broadcast_to(volume[:, None, :, None, :, None], (first, 2, second, 2, third, 2))
    return spread_out.reshape(2 * first, 2 * second, 2 * third)


def adjacent_cell_pairs(volume):
    padded = jnp.pad(volume, 1)
    return [padded[2:, 1:-1, 1:-1], padded[:-2, 1:-1, 1:-1], padded[1:-1, 2:, 1:-1],
            padded[1:-1, :-2, 1:-1], padded[1:-1, 1:-1, 2:], padded[1:-1, 1:-1, :-2]]


def accumulate_terms(summand_terms):
    summed_total = summand_terms[0]
    for summand_term in summand_terms[1:]:
        summed_total = summed_total + summand_term
    return summed_total


def mobilities(saturation, water_end, oil_end):
    water_mobility = water_end * saturation * saturation / mu_water
    oil_mobility = oil_end * (1.0 - saturation) * (1.0 - saturation) / mu_oil
    return water_mobility, oil_mobility


def fractional(saturation, water_end, oil_end):
    water_mobility, oil_mobility = mobilities(saturation, water_end, oil_end)
    mobility = water_mobility + oil_mobility
    water_slope = 2.0 * water_end * saturation / mu_water
    oil_slope = -2.0 * oil_end * (1.0 - saturation) / mu_oil
    return water_mobility / mobility, (water_slope * oil_mobility - water_mobility * oil_slope) / (mobility * mobility)


def upwind(frac, frac_beyond, outflows):
    return accumulate_terms([jnp.maximum(outward, 0.0) * frac + jnp.minimum(outward, 0.0) * exceeding_part
                    for outward, exceeding_part in zip(outflows, frac_beyond)])


def fine_step(sat_old, permeability, porosity, source_rate, water_end, oil_end):
    water_mobility, oil_mobility = mobilities(sat_old, water_end, oil_end)
    transport_field = permeability * (water_mobility + oil_mobility)
    transmissibility = [0.5 * (transport_field + exceeding_part) for exceeding_part in adjacent_cell_pairs(transport_field)]
    diagonal = compress + accumulate_terms(transmissibility)

    def operate(vector):
        return diagonal * vector - accumulate_terms([conduct_face * exceeding_part for conduct_face, exceeding_part in zip(transmissibility, adjacent_cell_pairs(vector))])

    solution = jnp.zeros_like(source_rate)
    residual = source_rate
    precond = residual / diagonal
    direction = precond
    rho_now = jnp.sum(residual * precond)
    for sweep_no in range(CG_ITERS):
        applied = operate(direction)
        step_len = rho_now / jnp.sum(direction * applied)
        solution = solution + step_len * direction
        if sweep_no + 1 < CG_ITERS:
            residual = residual - step_len * applied
            precond = residual / diagonal
            rho_next = jnp.sum(residual * precond)
            direction = precond + (rho_next / rho_now) * direction
            rho_now = rho_next
    pressure = solution
    outflows = [conduct_face * (pressure - exceeding_part) for conduct_face, exceeding_part in zip(transmissibility, adjacent_cell_pairs(pressure))]
    outgoing = accumulate_terms([jnp.maximum(outward, 0.0) for outward in outflows])
    saturation = sat_old
    for newton_no in range(NEWTON):
        frac, frac_slope = fractional(saturation, water_end, oil_end)
        flux_sum = upwind(frac, adjacent_cell_pairs(frac), outflows)
        balance = porosity * (saturation - sat_old) / step_dt + flux_sum - jnp.maximum(source_rate, 0.0) - jnp.minimum(source_rate, 0.0) * frac
        slope_sum = porosity / step_dt + jnp.abs(frac_slope) * (outgoing + jnp.maximum(-source_rate, 0.0))
        saturation = saturation - balance / slope_sum
    return saturation, pressure


def reference(initial_saturation, permeability, porosity, source_rate, rock_type, water_endpoint, oil_endpoint):
    water_coarse = lookup(rock_type, water_endpoint)
    oil_coarse = lookup(rock_type, oil_endpoint)
    water_fine = prolong(water_coarse)
    oil_fine = prolong(oil_coarse)
    start_coarse = restrict(initial_saturation)
    permeability_upscaled = restrict(permeability)
    poro_coarse = restrict(porosity)
    source_coarse = restrict(source_rate)

    water_mobility, oil_mobility = mobilities(start_coarse, water_coarse, oil_coarse)
    transport_field_upscaled = permeability_upscaled * (water_mobility + oil_mobility)
    transmissibility_upscaled = [(transport_field_upscaled + exceeding_part) / 8.0 for exceeding_part in adjacent_cell_pairs(transport_field_upscaled)]
    diag_coarse = compress + accumulate_terms(transmissibility_upscaled)
    pressure_coarse = damping * source_coarse / diag_coarse
    for sweep_no in range(SWEEPS - 1):
        coupled = accumulate_terms([conduct_face * exceeding_part for conduct_face, exceeding_part in zip(transmissibility_upscaled, adjacent_cell_pairs(pressure_coarse))])
        pressure_coarse = pressure_coarse + damping * (source_coarse - (diag_coarse * pressure_coarse - coupled)) / diag_coarse
    flows_coarse = [conduct_face * (pressure_coarse - exceeding_part) for conduct_face, exceeding_part in zip(transmissibility_upscaled, adjacent_cell_pairs(pressure_coarse))]
    outgoing_coarse = accumulate_terms([jnp.maximum(outward, 0.0) for outward in flows_coarse])
    coarse_dt = FSTEPS * step_dt

    def coarse_step(coarse_state):
        frac, frac_slope = fractional(coarse_state, water_coarse, oil_coarse)
        flux_sum = upwind(frac, adjacent_cell_pairs(frac), flows_coarse)
        balance = flux_sum - jnp.maximum(source_coarse, 0.0) - jnp.minimum(source_coarse, 0.0) * frac
        slope_sum = poro_coarse / coarse_dt + jnp.abs(frac_slope) * (outgoing_coarse + jnp.maximum(-source_coarse, 0.0))
        return coarse_state - balance / slope_sum

    def fine_prop(saturation):
        pressure = jnp.zeros_like(saturation)
        for fine_no in range(FSTEPS):
            saturation, pressure = fine_step(saturation, permeability, porosity, source_rate, water_fine, oil_fine)
        return saturation, pressure

    def chain(corrections):
        states = [start_coarse]
        images = []
        for slice_no in range(SLICES):
            coarse_image = coarse_step(states[slice_no])
            images.append(coarse_image)
            if corrections is None:
                states.append(coarse_image)
            else:
                states.append(coarse_image + corrections[slice_no])
        return states, images

    states, images = chain(None)
    starts = [initial_saturation] + [prolong(states[slice_no]) for slice_no in range(1, SLICES)]
    previous = images
    results = []
    ends = []
    for parareal_no in range(PARAREAL):
        results = [fine_prop(starts[slice_no]) for slice_no in range(SLICES)]
        corrections = [restrict(results[slice_no][0]) - previous[slice_no] for slice_no in range(SLICES)]
        states, images = chain(corrections)
        ends = [prolong(images[slice_no]) + results[slice_no][0] - prolong(previous[slice_no]) for slice_no in range(SLICES)]
        starts = [initial_saturation] + ends[:-1]
        previous = images
    return jnp.stack(ends), jnp.stack([results[slice_no][1] for slice_no in range(SLICES)])
```

```python
import jax
import jax.numpy as jnp
from jax import lax
from jax.sharding import PartitionSpec as P

FSTEPS = 1
NEWTON = 2
CG_ITERS = 3
SWEEPS = 3
PARAREAL = 2
ROCKS = 4


mu_water = 1.0
mu_oil = 4.0
compress = 0.05
step_dt = 0.25
damping = 0.8


def extended(array, sides, width):
    for axis, dim in sides:
        size, length = (lax.axis_size(axis), array.shape[dim])
        up = [(i, (i + 1) % size) for i in range(size - 1)]
        down = [(j, i) for i, j in up]
        last = lax.slice_in_dim(array, length - width, length, axis=dim)
        initial = lax.slice_in_dim(array, 0, width, axis=dim)
        before = lax.ppermute(last, axis, up)
        after = lax.ppermute(initial, axis, down)
        array = jnp.concatenate([before, array, after], axis=dim)
    return array


def passed_along(value, axis, steps):
    count = lax.axis_size(axis)
    initial, last = (max(0, -steps), min(count, count - steps))
    return lax.ppermute(value, axis, [(source, source + steps) for source in range(initial, last)])


def lookup(rock_cells, end_values):
    summed_total = jnp.zeros(rock_cells.shape, end_values.dtype)
    for rock_kind in range(ROCKS):
        summed_total = summed_total + jnp.where(
            rock_cells == rock_kind, end_values[rock_kind], jnp.zeros((), end_values.dtype)
        )
    return summed_total


def restrict(volume):
    return volume.reshape(
        volume.shape[0] // 2, 2, volume.shape[1] // 2, 2, volume.shape[2] // 2, 2
    ).mean(axis=(1, 3, 5))


def prolong(volume):
    first, second, third = volume.shape
    spread_out = jnp.broadcast_to(
        volume[:, None, :, None, :, None], (first, 2, second, 2, third, 2)
    )
    return spread_out.reshape(2 * first, 2 * second, 2 * third)


def pad_depth(volume):
    return jnp.pad(volume, ((0, 0), (0, 0), (1, 1)))


def face_list(padded):
    return [
        padded[2:, 1:-1, 1:-1],
        padded[:-2, 1:-1, 1:-1],
        padded[1:-1, 2:, 1:-1],
        padded[1:-1, :-2, 1:-1],
        padded[1:-1, 1:-1, 2:],
        padded[1:-1, 1:-1, :-2],
    ]


def face_mobility_values(volume):
    return face_list(pad_depth(extended(volume, (("sx", 0), ("sy", 1)), 1)))


def direction_spread(volume):
    return extended(volume, (("sx", 0), ("sy", 1)), 1)


def pressure_faces(volume):
    return face_list(pad_depth(extended(volume, (("sx", 0), ("sy", 1)), 1)))


def flow_faces(volume):
    return face_list(pad_depth(extended(volume, (("sx", 0), ("sy", 1)), 1)))


def build_face_tables(volume):
    return face_list(pad_depth(extended(volume, (("sx", 0), ("sy", 1)), 1)))


def coarse_faces(volume):
    return face_list(pad_depth(extended(volume, (("sx", 0), ("sy", 1)), 1)))


def accumulate_terms(summand_terms):
    summed_total = summand_terms[0]
    for summand_term in summand_terms[1:]:
        summed_total = summed_total + summand_term
    return summed_total


def mobilities(saturation, water_end, oil_end):
    water_mobility = water_end * saturation * saturation / mu_water
    oil_mobility = oil_end * (1.0 - saturation) * (1.0 - saturation) / mu_oil
    return (water_mobility, oil_mobility)


def fractional(saturation, water_end, oil_end):
    water_mobility, oil_mobility = mobilities(saturation, water_end, oil_end)
    mobility = water_mobility + oil_mobility
    water_slope = 2.0 * water_end * saturation / mu_water
    oil_slope = -2.0 * oil_end * (1.0 - saturation) / mu_oil
    return (
        water_mobility / mobility,
        (water_slope * oil_mobility - water_mobility * oil_slope) / (mobility * mobility),
    )


def upwind(frac, frac_beyond, outflows):
    return accumulate_terms(
        [
            jnp.maximum(outward, 0.0) * frac + jnp.minimum(outward, 0.0) * exceeding_part
            for outward, exceeding_part in zip(outflows, frac_beyond)
        ]
    )


def global_sums(values):
    count = lax.axis_size("sx") * lax.axis_size("sy")
    packed = jnp.broadcast_to(jnp.stack(values)[None], (count, len(values)))
    gathered = lax.all_to_all(packed, ("sx", "sy"), 0, 0, tiled=True)
    totals = jnp.sum(gathered, axis=0)
    return [totals[k] for k in range(len(values))]


def apply_operator(diagonal, transmissibility, vector):
    spread_vec = direction_spread(vector)
    return diagonal * vector - accumulate_terms(
        [
            conduct_face * exceeding_part
            for conduct_face, exceeding_part in zip(transmissibility, face_list(pad_depth(spread_vec)))
        ]
    )


def solve_pressure(source_rate, diagonal, transmissibility):
    residual = source_rate
    solution = None
    for sweep_no in range(CG_ITERS):
        precond = residual / diagonal
        image = apply_operator(diagonal, transmissibility, precond)
        rho_next, curvature = global_sums([jnp.sum(residual * precond), jnp.sum(precond * image)])
        if sweep_no == 0:
            step_len = rho_next / curvature
            direction = precond
            applied = image
            solution = step_len * direction
        else:
            ratio = rho_next / rho_now
            step_len = rho_next / (curvature - ratio * rho_next / step_len)
            direction = precond + ratio * direction
            applied = image + ratio * applied
            solution = solution + step_len * direction
        if sweep_no + 1 < CG_ITERS:
            residual = residual - step_len * applied
        rho_now = rho_next
    return solution


def fine_step(sat_old, permeability, porosity, source_rate, water_end, oil_end):
    water_mobility, oil_mobility = mobilities(sat_old, water_end, oil_end)
    transport_field = permeability * (water_mobility + oil_mobility)
    transmissibility = [
        0.5 * (transport_field + exceeding_part)
        for exceeding_part in face_mobility_values(transport_field)
    ]
    diagonal = compress + accumulate_terms(transmissibility)
    pressure = solve_pressure(source_rate, diagonal, transmissibility)
    beside = pressure_faces(pressure)
    outflows = [
        conduct_face * (pressure - exceeding_part)
        for conduct_face, exceeding_part in zip(transmissibility, beside)
    ]
    outgoing = accumulate_terms([jnp.maximum(outward, 0.0) for outward in outflows])
    saturation = sat_old
    for newton_no in range(NEWTON):
        frac, frac_slope = fractional(saturation, water_end, oil_end)
        flux_sum = upwind(frac, flow_faces(frac), outflows)
        balance = (
            porosity * (saturation - sat_old) / step_dt
            + flux_sum
            - jnp.maximum(source_rate, 0.0)
            - jnp.minimum(source_rate, 0.0) * frac
        )
        slope_sum = porosity / step_dt + jnp.abs(frac_slope) * (
            outgoing + jnp.maximum(-source_rate, 0.0)
        )
        saturation = saturation - balance / slope_sum
    return (saturation, pressure)


def local(
    initial_saturation, permeability, porosity, source_rate, rock_type, water_endpoint, oil_endpoint
):
    slices = lax.axis_size("tm")
    slice_index = lax.axis_index("tm")
    water_coarse = lookup(rock_type, water_endpoint)
    oil_coarse = lookup(rock_type, oil_endpoint)
    water_fine = prolong(water_coarse)
    oil_fine = prolong(oil_coarse)
    start_coarse = restrict(initial_saturation)
    permeability_upscaled = restrict(permeability)
    poro_coarse = restrict(porosity)
    source_coarse = restrict(source_rate)
    water_mobility, oil_mobility = mobilities(start_coarse, water_coarse, oil_coarse)
    transport_field_upscaled = permeability_upscaled * (water_mobility + oil_mobility)
    transmissibility_upscaled = [
        (transport_field_upscaled + exceeding_part) / 8.0
        for exceeding_part in build_face_tables(transport_field_upscaled)
    ]
    diag_coarse = compress + accumulate_terms(transmissibility_upscaled)
    pressure_coarse = damping * source_coarse / diag_coarse
    for sweep_no in range(SWEEPS):
        beside = build_face_tables(pressure_coarse)
        if sweep_no + 1 < SWEEPS:
            coupled = accumulate_terms(
                [
                    conduct_face * exceeding_part
                    for conduct_face, exceeding_part in zip(transmissibility_upscaled, beside)
                ]
            )
            pressure_coarse = (
                pressure_coarse
                + damping
                * (source_coarse - (diag_coarse * pressure_coarse - coupled))
                / diag_coarse
            )
    flows_coarse = [
        conduct_face * (pressure_coarse - exceeding_part)
        for conduct_face, exceeding_part in zip(transmissibility_upscaled, beside)
    ]
    outgoing_coarse = accumulate_terms([jnp.maximum(outward, 0.0) for outward in flows_coarse])
    coarse_dt = FSTEPS * step_dt

    def coarse_step(coarse_state):
        frac, frac_slope = fractional(coarse_state, water_coarse, oil_coarse)
        flux_sum = upwind(frac, coarse_faces(frac), flows_coarse)
        balance = (
            flux_sum - jnp.maximum(source_coarse, 0.0) - jnp.minimum(source_coarse, 0.0) * frac
        )
        slope_sum = poro_coarse / coarse_dt + jnp.abs(frac_slope) * (
            outgoing_coarse + jnp.maximum(-source_coarse, 0.0)
        )
        return coarse_state - balance / slope_sum

    def chain(corrections):

        def relay_round(turn_no, coarse_state):
            coarse_image = coarse_step(coarse_state)
            if corrections is None:
                outgoing_state = coarse_image
            else:
                outgoing_state = coarse_image + corrections
            arrived = passed_along(outgoing_state, "tm", 1)
            return jnp.where(slice_index == 0, start_coarse, arrived)

        coarse_state = lax.fori_loop(0, slices - 1, relay_round, start_coarse)
        return (coarse_state, coarse_step(coarse_state))

    coarse_state, coarse_image = chain(None)
    starts = jnp.where(slice_index == 0, initial_saturation, prolong(coarse_state))
    previous_image = coarse_image
    ends = starts
    pressure = starts
    for parareal_no in range(PARAREAL):
        saturation = starts
        saturation, fine_pressure = fine_step(
            saturation, permeability, porosity, source_rate, water_fine, oil_fine
        )
        pressure = fine_pressure
        corrections = restrict(saturation) - previous_image
        coarse_state, coarse_image = chain(corrections)
        ends = prolong(coarse_image) + saturation - prolong(previous_image)
        if parareal_no + 1 < PARAREAL:
            arrived_start = passed_along(ends, "tm", 1)
            starts = jnp.where(slice_index == 0, initial_saturation, arrived_start)
        previous_image = coarse_image
    return (ends[None], pressure[None])


def solution(mesh):
    in_specs = (
        P("sx", "sy", None),
        P("sx", "sy", None),
        P("sx", "sy", None),
        P("sx", "sy", None),
        P("sx", "sy", None),
        P(),
        P(),
    )
    out_specs = (P("tm", "sx", "sy", None), P("tm", "sx", "sy", None))
    return jax.shard_map(local, mesh=mesh, in_specs=in_specs, out_specs=out_specs, check_vma=False)
```

```python
import jax
import jax.numpy as jnp
from jax import lax
from jax.sharding import PartitionSpec as P

FSTEPS = 1
NEWTON = 2
CG_ITERS = 3
SWEEPS = 3
PARAREAL = 2
ROCKS = 4


mu_water = 1.0
mu_oil = 4.0
compress = 0.05
step_dt = 0.25
damping = 0.8


def extended(array, sides, width):
    for axis, dim in sides:
        size, length = (lax.axis_size(axis), array.shape[dim])
        up = [(i, (i + 1) % size) for i in range(size - 1)]
        down = [(j, i) for i, j in up]
        last = lax.slice_in_dim(array, length - width, length, axis=dim)
        initial = lax.slice_in_dim(array, 0, width, axis=dim)
        before = lax.ppermute(last, axis, up)
        after = lax.ppermute(initial, axis, down)
        array = jnp.concatenate([before, array, after], axis=dim)
    return array


def passed_along(value, axis, steps):
    count = lax.axis_size(axis)
    initial, last = (max(0, -steps), min(count, count - steps))
    return lax.ppermute(value, axis, [(source, source + steps) for source in range(initial, last)])


def lookup(rock_cells, end_values):
    summed_total = jnp.zeros(rock_cells.shape, end_values.dtype)
    for rock_kind in range(ROCKS):
        summed_total = summed_total + jnp.where(
            rock_cells == rock_kind, end_values[rock_kind], jnp.zeros((), end_values.dtype)
        )
    return summed_total


def restrict(volume):
    return volume.reshape(
        volume.shape[0] // 2, 2, volume.shape[1] // 2, 2, volume.shape[2] // 2, 2
    ).mean(axis=(1, 3, 5))


def prolong(volume):
    first, second, third = volume.shape
    spread_out = jnp.broadcast_to(
        volume[:, None, :, None, :, None], (first, 2, second, 2, third, 2)
    )
    return spread_out.reshape(2 * first, 2 * second, 2 * third)


def pad_depth(volume):
    return jnp.pad(volume, ((0, 0), (0, 0), (1, 1)))


def face_list(padded):
    return [
        padded[2:, 1:-1, 1:-1],
        padded[:-2, 1:-1, 1:-1],
        padded[1:-1, 2:, 1:-1],
        padded[1:-1, :-2, 1:-1],
        padded[1:-1, 1:-1, 2:],
        padded[1:-1, 1:-1, :-2],
    ]


def face_mobility_values(volume):
    return face_list(pad_depth(extended(volume, (("sx", 0), ("sy", 1)), 1)))


def direction_spread(volume):
    return extended(volume, (("sx", 0), ("sy", 1)), 1)


def pressure_faces(volume):
    return face_list(pad_depth(extended(volume, (("sx", 0), ("sy", 1)), 1)))


def flow_faces(volume):
    return face_list(pad_depth(extended(volume, (("sx", 0), ("sy", 1)), 1)))


def build_face_tables(volume):
    return face_list(pad_depth(extended(volume, (("sx", 0), ("sy", 1)), 1)))


def coarse_faces(volume):
    return face_list(pad_depth(extended(volume, (("sx", 0), ("sy", 1)), 1)))


def accumulate_terms(summand_terms):
    summed_total = summand_terms[0]
    for summand_term in summand_terms[1:]:
        summed_total = summed_total + summand_term
    return summed_total


def mobilities(saturation, water_end, oil_end):
    water_mobility = water_end * saturation * saturation / mu_water
    oil_mobility = oil_end * (1.0 - saturation) * (1.0 - saturation) / mu_oil
    return (water_mobility, oil_mobility)


def fractional(saturation, water_end, oil_end):
    water_mobility, oil_mobility = mobilities(saturation, water_end, oil_end)
    mobility = water_mobility + oil_mobility
    water_slope = 2.0 * water_end * saturation / mu_water
    oil_slope = -2.0 * oil_end * (1.0 - saturation) / mu_oil
    return (
        water_mobility / mobility,
        (water_slope * oil_mobility - water_mobility * oil_slope) / (mobility * mobility),
    )


def upwind(frac, frac_beyond, outflows):
    return accumulate_terms(
        [
            jnp.maximum(outward, 0.0) * frac + jnp.minimum(outward, 0.0) * exceeding_part
            for outward, exceeding_part in zip(outflows, frac_beyond)
        ]
    )


def global_sums(values):
    count = lax.axis_size("sx") * lax.axis_size("sy")
    packed = jnp.broadcast_to(jnp.stack(values)[None], (count, len(values)))
    gathered = lax.all_to_all(packed, ("sx", "sy"), 0, 0, tiled=True)
    totals = jnp.sum(gathered, axis=0)
    return [totals[k] for k in range(len(values))]


def apply_operator(diagonal, transmissibility, vector):
    spread_vec = direction_spread(vector)
    return diagonal * vector - accumulate_terms(
        [
            conduct_face * exceeding_part
            for conduct_face, exceeding_part in zip(transmissibility, face_list(pad_depth(spread_vec)))
        ]
    )


def solve_pressure(source_rate, diagonal, transmissibility):
    residual = source_rate
    solution = None
    for sweep_no in range(CG_ITERS):
        precond = residual / diagonal
        image = apply_operator(diagonal, transmissibility, precond)
        rho_next, curvature = global_sums([jnp.sum(residual * precond), jnp.sum(precond * image)])
        if sweep_no == 0:
            step_len = rho_next / curvature
            direction = precond
            applied = image
            solution = step_len * direction
        else:
            ratio = rho_next / rho_now
            step_len = rho_next / (curvature - ratio * rho_next / step_len)
            direction = precond + ratio * direction
            applied = image + ratio * applied
            solution = solution + step_len * direction
        if sweep_no + 1 < CG_ITERS:
            residual = residual - step_len * applied
        rho_now = rho_next
    return solution


def fine_step(sat_old, permeability, porosity, source_rate, water_end, oil_end):
    water_mobility, oil_mobility = mobilities(sat_old, water_end, oil_end)
    transport_field = permeability * (water_mobility + oil_mobility)
    transmissibility = [
        0.5 * (transport_field + exceeding_part)
        for exceeding_part in face_mobility_values(transport_field)
    ]
    diagonal = compress + accumulate_terms(transmissibility)
    pressure = solve_pressure(source_rate, diagonal, transmissibility)
    beside = pressure_faces(pressure)
    outflows = [
        conduct_face * (pressure - exceeding_part)
        for conduct_face, exceeding_part in zip(transmissibility, beside)
    ]
    outgoing = accumulate_terms([jnp.maximum(outward, 0.0) for outward in outflows])
    saturation = sat_old
    for newton_no in range(NEWTON):
        frac, frac_slope = fractional(saturation, water_end, oil_end)
        flux_sum = upwind(frac, flow_faces(frac), outflows)
        balance = (
            porosity * (saturation - sat_old) / step_dt
            + flux_sum
            - jnp.maximum(source_rate, 0.0)
            - jnp.minimum(source_rate, 0.0) * frac
        )
        slope_sum = porosity / step_dt + jnp.abs(frac_slope) * (
            outgoing + jnp.maximum(-source_rate, 0.0)
        )
        saturation = saturation - balance / slope_sum
    return (saturation, pressure)


def gather_grid(blocks):
    rows, cols = (lax.axis_size("sx"), lax.axis_size("sy"))
    packed = jnp.broadcast_to(blocks[None], (rows * cols,) + blocks.shape)
    gathered = lax.all_to_all(packed, ("sx", "sy"), 0, 0, tiled=True)
    fields, depth_x, depth_y, depth_z = blocks.shape
    gathered = gathered.reshape(rows, cols, fields, depth_x, depth_y, depth_z)
    gathered = gathered.transpose(2, 0, 3, 1, 4, 5)
    return gathered.reshape(fields, rows * depth_x, cols * depth_y, depth_z)


def own_block(whole, shape):
    corner = (lax.axis_index("sx") * shape[0], lax.axis_index("sy") * shape[1], 0)
    return lax.dynamic_slice(whole, corner, shape)


def whole_faces(volume):
    return face_list(jnp.pad(volume, 1))


def local(
    initial_saturation, permeability, porosity, source_rate, rock_type, water_endpoint, oil_endpoint
):
    slices = lax.axis_size("tm")
    slice_index = lax.axis_index("tm")
    water_block = lookup(rock_type, water_endpoint)
    oil_block = lookup(rock_type, oil_endpoint)
    water_fine = prolong(water_block)
    oil_fine = prolong(oil_block)
    start_block = restrict(initial_saturation)
    block_shape = start_block.shape
    whole = gather_grid(
        jnp.stack(
            [
                start_block,
                restrict(permeability),
                restrict(porosity),
                restrict(source_rate),
                water_block,
                oil_block,
            ]
        )
    )
    start_coarse, permeability_upscaled, poro_coarse, source_coarse, water_coarse, oil_coarse = (
        whole[k] for k in range(6)
    )
    water_mobility, oil_mobility = mobilities(start_coarse, water_coarse, oil_coarse)
    transport_field_upscaled = permeability_upscaled * (water_mobility + oil_mobility)
    transmissibility_upscaled = [
        (transport_field_upscaled + exceeding_part) / 8.0
        for exceeding_part in whole_faces(transport_field_upscaled)
    ]
    diag_coarse = compress + accumulate_terms(transmissibility_upscaled)
    pressure_coarse = damping * source_coarse / diag_coarse
    for sweep_no in range(SWEEPS - 1):
        coupled = accumulate_terms(
            [
                conduct_face * exceeding_part
                for conduct_face, exceeding_part in zip(
                    transmissibility_upscaled, whole_faces(pressure_coarse)
                )
            ]
        )
        pressure_coarse = (
            pressure_coarse
            + damping * (source_coarse - (diag_coarse * pressure_coarse - coupled)) / diag_coarse
        )
    flows_coarse = [
        conduct_face * (pressure_coarse - exceeding_part)
        for conduct_face, exceeding_part in zip(transmissibility_upscaled, whole_faces(pressure_coarse))
    ]
    outgoing_coarse = accumulate_terms([jnp.maximum(outward, 0.0) for outward in flows_coarse])
    coarse_dt = FSTEPS * step_dt

    def coarse_step(coarse_state):
        frac, frac_slope = fractional(coarse_state, water_coarse, oil_coarse)
        flux_sum = upwind(frac, whole_faces(frac), flows_coarse)
        balance = (
            flux_sum - jnp.maximum(source_coarse, 0.0) - jnp.minimum(source_coarse, 0.0) * frac
        )
        slope_sum = poro_coarse / coarse_dt + jnp.abs(frac_slope) * (
            outgoing_coarse + jnp.maximum(-source_coarse, 0.0)
        )
        return coarse_state - balance / slope_sum

    def chain(corrections):

        def relay_round(turn_no, coarse_state):
            coarse_image = coarse_step(coarse_state)
            if corrections is None:
                outgoing_state = coarse_image
            else:
                outgoing_state = coarse_image + corrections
            arrived = passed_along(outgoing_state, "tm", 1)
            return jnp.where(slice_index == 0, start_coarse, arrived)

        coarse_state = lax.fori_loop(0, slices - 1, relay_round, start_coarse)
        return (coarse_state, coarse_step(coarse_state))

    coarse_state, coarse_image = chain(None)
    starts = jnp.where(
        slice_index == 0, initial_saturation, prolong(own_block(coarse_state, block_shape))
    )
    previous_image = coarse_image
    ends = starts
    pressure = starts
    for parareal_no in range(PARAREAL):
        saturation = starts
        saturation, fine_pressure = fine_step(
            saturation, permeability, porosity, source_rate, water_fine, oil_fine
        )
        pressure = fine_pressure
        corrections = gather_grid(restrict(saturation)[None])[0] - previous_image
        coarse_state, coarse_image = chain(corrections)
        ends = (
            prolong(own_block(coarse_image, block_shape))
            + saturation
            - prolong(own_block(previous_image, block_shape))
        )
        if parareal_no + 1 < PARAREAL:
            arrived_start = passed_along(ends, "tm", 1)
            starts = jnp.where(slice_index == 0, initial_saturation, arrived_start)
        previous_image = coarse_image
    return (ends[None], pressure[None])


def solution(mesh):
    in_specs = (
        P("sx", "sy", None),
        P("sx", "sy", None),
        P("sx", "sy", None),
        P("sx", "sy", None),
        P("sx", "sy", None),
        P(),
        P(),
    )
    out_specs = (P("tm", "sx", "sy", None), P("tm", "sx", "sy", None))
    return jax.shard_map(local, mesh=mesh, in_specs=in_specs, out_specs=out_specs, check_vma=False)
```

```python
import jax
import jax.numpy as jnp
from jax import lax
from jax.sharding import PartitionSpec as P

FSTEPS = 1
NEWTON = 2
CG_ITERS = 3
SWEEPS = 3
PARAREAL = 2
ROCKS = 4


mu_water = 1.0
mu_oil = 4.0
compress = 0.05
step_dt = 0.25
damping = 0.8


def extended(array, sides, width):
    for axis, dim in sides:
        size, length = (lax.axis_size(axis), array.shape[dim])
        up = [(i, (i + 1) % size) for i in range(size - 1)]
        down = [(j, i) for i, j in up]
        last = lax.slice_in_dim(array, length - width, length, axis=dim)
        initial = lax.slice_in_dim(array, 0, width, axis=dim)
        before = lax.ppermute(last, axis, up)
        after = lax.ppermute(initial, axis, down)
        array = jnp.concatenate([before, array, after], axis=dim)
    return array


def passed_along(value, axis, steps):
    count = lax.axis_size(axis)
    initial, last = (max(0, -steps), min(count, count - steps))
    return lax.ppermute(value, axis, [(source, source + steps) for source in range(initial, last)])


def lookup(rock_cells, end_values):
    summed_total = jnp.zeros(rock_cells.shape, end_values.dtype)
    for rock_kind in range(ROCKS):
        summed_total = summed_total + jnp.where(
            rock_cells == rock_kind, end_values[rock_kind], jnp.zeros((), end_values.dtype)
        )
    return summed_total


def restrict(volume):
    return volume.reshape(
        volume.shape[0] // 2, 2, volume.shape[1] // 2, 2, volume.shape[2] // 2, 2
    ).mean(axis=(1, 3, 5))


def prolong(volume):
    first, second, third = volume.shape
    spread_out = jnp.broadcast_to(
        volume[:, None, :, None, :, None], (first, 2, second, 2, third, 2)
    )
    return spread_out.reshape(2 * first, 2 * second, 2 * third)


def pad_depth(volume):
    return jnp.pad(volume, ((0, 0), (0, 0), (1, 1)))


def face_list(padded):
    return [
        padded[2:, 1:-1, 1:-1],
        padded[:-2, 1:-1, 1:-1],
        padded[1:-1, 2:, 1:-1],
        padded[1:-1, :-2, 1:-1],
        padded[1:-1, 1:-1, 2:],
        padded[1:-1, 1:-1, :-2],
    ]


ROW_AXES = ("sx", "sy")


def row_halo(volume):
    count = lax.axis_size("sx") * lax.axis_size("sy")
    up = [(i, i + 1) for i in range(count - 1)]
    down = [(i + 1, i) for i in range(count - 1)]
    before = lax.ppermute(volume[-1:], ROW_AXES, up)
    after = lax.ppermute(volume[:1], ROW_AXES, down)
    return jnp.concatenate([before, volume, after], axis=0)


def row_faces(volume):
    return face_list(jnp.pad(row_halo(volume), ((0, 0), (1, 1), (1, 1))))


def face_mobility_values(volume):
    return row_faces(volume)


def direction_spread(volume):
    return extended(volume, (("sx", 0), ("sy", 1)), 1)


def pressure_faces(volume):
    return row_faces(volume)


def flow_faces(volume):
    return row_faces(volume)


def build_face_tables(volume):
    return face_list(pad_depth(extended(volume, (("sx", 0), ("sy", 1)), 1)))


def coarse_faces(volume):
    return face_list(pad_depth(extended(volume, (("sx", 0), ("sy", 1)), 1)))


def accumulate_terms(summand_terms):
    summed_total = summand_terms[0]
    for summand_term in summand_terms[1:]:
        summed_total = summed_total + summand_term
    return summed_total


def mobilities(saturation, water_end, oil_end):
    water_mobility = water_end * saturation * saturation / mu_water
    oil_mobility = oil_end * (1.0 - saturation) * (1.0 - saturation) / mu_oil
    return (water_mobility, oil_mobility)


def fractional(saturation, water_end, oil_end):
    water_mobility, oil_mobility = mobilities(saturation, water_end, oil_end)
    mobility = water_mobility + oil_mobility
    water_slope = 2.0 * water_end * saturation / mu_water
    oil_slope = -2.0 * oil_end * (1.0 - saturation) / mu_oil
    return (
        water_mobility / mobility,
        (water_slope * oil_mobility - water_mobility * oil_slope) / (mobility * mobility),
    )


def upwind(frac, frac_beyond, outflows):
    return accumulate_terms(
        [
            jnp.maximum(outward, 0.0) * frac + jnp.minimum(outward, 0.0) * exceeding_part
            for outward, exceeding_part in zip(outflows, frac_beyond)
        ]
    )


def global_sums(values):
    count = lax.axis_size("sx") * lax.axis_size("sy")
    packed = jnp.broadcast_to(jnp.stack(values)[None], (count, len(values)))
    gathered = lax.all_to_all(packed, ("sx", "sy"), 0, 0, tiled=True)
    totals = jnp.sum(gathered, axis=0)
    return [totals[k] for k in range(len(values))]


def apply_operator(diagonal, transmissibility, vector):
    return diagonal * vector - accumulate_terms(
        [
            conduct_face * exceeding_part
            for conduct_face, exceeding_part in zip(transmissibility, row_faces(vector))
        ]
    )


def solve_pressure(source_rate, diagonal, transmissibility):
    residual = source_rate
    solution = None
    for sweep_no in range(CG_ITERS):
        precond = residual / diagonal
        image = apply_operator(diagonal, transmissibility, precond)
        rho_next, curvature = global_sums([jnp.sum(residual * precond), jnp.sum(precond * image)])
        if sweep_no == 0:
            step_len = rho_next / curvature
            direction = precond
            applied = image
            solution = step_len * direction
        else:
            ratio = rho_next / rho_now
            step_len = rho_next / (curvature - ratio * rho_next / step_len)
            direction = precond + ratio * direction
            applied = image + ratio * applied
            solution = solution + step_len * direction
        if sweep_no + 1 < CG_ITERS:
            residual = residual - step_len * applied
        rho_now = rho_next
    return solution


def fine_step(sat_old, permeability, porosity, source_rate, water_end, oil_end):
    water_mobility, oil_mobility = mobilities(sat_old, water_end, oil_end)
    transport_field = permeability * (water_mobility + oil_mobility)
    transmissibility = [
        0.5 * (transport_field + exceeding_part)
        for exceeding_part in face_mobility_values(transport_field)
    ]
    diagonal = compress + accumulate_terms(transmissibility)
    pressure = solve_pressure(source_rate, diagonal, transmissibility)
    beside = pressure_faces(pressure)
    outflows = [
        conduct_face * (pressure - exceeding_part)
        for conduct_face, exceeding_part in zip(transmissibility, beside)
    ]
    outgoing = accumulate_terms([jnp.maximum(outward, 0.0) for outward in outflows])
    saturation = sat_old
    for newton_no in range(NEWTON):
        frac, frac_slope = fractional(saturation, water_end, oil_end)
        flux_sum = upwind(frac, flow_faces(frac), outflows)
        balance = (
            porosity * (saturation - sat_old) / step_dt
            + flux_sum
            - jnp.maximum(source_rate, 0.0)
            - jnp.minimum(source_rate, 0.0) * frac
        )
        slope_sum = porosity / step_dt + jnp.abs(frac_slope) * (
            outgoing + jnp.maximum(-source_rate, 0.0)
        )
        saturation = saturation - balance / slope_sum
    return (saturation, pressure)


def gather_grid(blocks):
    rows, cols = (lax.axis_size("sx"), lax.axis_size("sy"))
    packed = jnp.broadcast_to(blocks[None], (rows * cols,) + blocks.shape)
    gathered = lax.all_to_all(packed, ("sx", "sy"), 0, 0, tiled=True)
    fields, depth_x, depth_y, depth_z = blocks.shape
    gathered = gathered.reshape(rows, cols, fields, depth_x, depth_y, depth_z)
    gathered = gathered.transpose(2, 0, 3, 1, 4, 5)
    return gathered.reshape(fields, rows * depth_x, cols * depth_y, depth_z)


def own_block(whole, shape):
    corner = (lax.axis_index("sx") * shape[0], lax.axis_index("sy") * shape[1], 0)
    return lax.dynamic_slice(whole, corner, shape)


def to_rows(blocks):
    columns = lax.axis_size("sy")
    fields, depth_x, depth_y, depth_z = blocks.shape
    share = depth_x // columns
    packed = blocks.reshape(fields, columns, share, depth_y, depth_z).transpose(1, 0, 2, 3, 4)
    got = lax.all_to_all(packed, "sy", 0, 0, tiled=True)
    return got.transpose(1, 2, 0, 3, 4).reshape(fields, share, columns * depth_y, depth_z)


def from_rows(rows):
    columns = lax.axis_size("sy")
    fields, share, length_y, depth_z = rows.shape
    depth_y = length_y // columns
    packed = rows.reshape(fields, share, columns, depth_y, depth_z).transpose(2, 0, 1, 3, 4)
    got = lax.all_to_all(packed, "sy", 0, 0, tiled=True)
    return got.transpose(1, 0, 2, 3, 4).reshape(fields, columns * share, depth_y, depth_z)


def row_index():
    return lax.axis_index("sx") * lax.axis_size("sy") + lax.axis_index("sy")


def restrict_rows(rows):
    share, length_y, depth_z = rows.shape
    partial = rows.reshape(share, length_y // 2, 2, depth_z // 2, 2).sum(axis=(2, 4))
    count = lax.axis_size("sx") * lax.axis_size("sy")
    packed = jnp.broadcast_to(partial[None], (count,) + partial.shape)
    gathered = lax.all_to_all(packed, ROW_AXES, 0, 0, tiled=True)
    gathered = gathered.reshape(count * share // 2, 2, length_y // 2, depth_z // 2)
    return gathered.sum(axis=1) / 8.0


def prolong_rows(whole, share):
    coarse_rows = (row_index() * share + jnp.arange(share)) // 2
    picked = jnp.take(whole, coarse_rows, axis=0)
    count, length_y, depth_z = picked.shape
    spread_out = jnp.broadcast_to(picked[:, :, None, :, None], (count, length_y, 2, depth_z, 2))
    return spread_out.reshape(count, 2 * length_y, 2 * depth_z)


def whole_faces(volume):
    return face_list(jnp.pad(volume, 1))


def local(
    initial_saturation, permeability, porosity, source_rate, rock_type, water_endpoint, oil_endpoint
):
    slices = lax.axis_size("tm")
    slice_index = lax.axis_index("tm")
    water_block = lookup(rock_type, water_endpoint)
    oil_block = lookup(rock_type, oil_endpoint)
    start_block = restrict(initial_saturation)
    block_shape = start_block.shape
    whole = gather_grid(
        jnp.stack(
            [
                start_block,
                restrict(permeability),
                restrict(porosity),
                restrict(source_rate),
                water_block,
                oil_block,
            ]
        )
    )
    start_coarse, permeability_upscaled, poro_coarse, source_coarse, water_coarse, oil_coarse = (
        whole[k] for k in range(6)
    )
    water_mobility, oil_mobility = mobilities(start_coarse, water_coarse, oil_coarse)
    transport_field_upscaled = permeability_upscaled * (water_mobility + oil_mobility)
    transmissibility_upscaled = [
        (transport_field_upscaled + exceeding_part) / 8.0
        for exceeding_part in whole_faces(transport_field_upscaled)
    ]
    diag_coarse = compress + accumulate_terms(transmissibility_upscaled)
    pressure_coarse = damping * source_coarse / diag_coarse
    for sweep_no in range(SWEEPS - 1):
        coupled = accumulate_terms(
            [
                conduct_face * exceeding_part
                for conduct_face, exceeding_part in zip(
                    transmissibility_upscaled, whole_faces(pressure_coarse)
                )
            ]
        )
        pressure_coarse = (
            pressure_coarse
            + damping * (source_coarse - (diag_coarse * pressure_coarse - coupled)) / diag_coarse
        )
    flows_coarse = [
        conduct_face * (pressure_coarse - exceeding_part)
        for conduct_face, exceeding_part in zip(transmissibility_upscaled, whole_faces(pressure_coarse))
    ]
    outgoing_coarse = accumulate_terms([jnp.maximum(outward, 0.0) for outward in flows_coarse])
    coarse_dt = FSTEPS * step_dt

    def coarse_step(coarse_state):
        frac, frac_slope = fractional(coarse_state, water_coarse, oil_coarse)
        flux_sum = upwind(frac, whole_faces(frac), flows_coarse)
        balance = (
            flux_sum - jnp.maximum(source_coarse, 0.0) - jnp.minimum(source_coarse, 0.0) * frac
        )
        slope_sum = poro_coarse / coarse_dt + jnp.abs(frac_slope) * (
            outgoing_coarse + jnp.maximum(-source_coarse, 0.0)
        )
        return coarse_state - balance / slope_sum

    def chain(corrections):

        def relay_round(turn_no, coarse_state):
            coarse_image = coarse_step(coarse_state)
            if corrections is None:
                outgoing_state = coarse_image
            else:
                outgoing_state = coarse_image + corrections
            arrived = passed_along(outgoing_state, "tm", 1)
            return jnp.where(slice_index == 0, start_coarse, arrived)

        coarse_state = lax.fori_loop(0, slices - 1, relay_round, start_coarse)
        return (coarse_state, coarse_step(coarse_state))

    initial_rows, permeability, porosity, source_rate, water_fine, oil_fine = to_rows(
        jnp.stack(
            [
                initial_saturation,
                permeability,
                porosity,
                source_rate,
                prolong(water_block),
                prolong(oil_block),
            ]
        )
    )
    share = initial_rows.shape[0]
    coarse_state, coarse_image = chain(None)
    starts = jnp.where(slice_index == 0, initial_rows, prolong_rows(coarse_state, share))
    previous_image = coarse_image
    ends = starts
    pressure = starts
    for parareal_no in range(PARAREAL):
        saturation = starts
        saturation, fine_pressure = fine_step(
            saturation, permeability, porosity, source_rate, water_fine, oil_fine
        )
        pressure = fine_pressure
        corrections = restrict_rows(saturation) - previous_image
        coarse_state, coarse_image = chain(corrections)
        ends = prolong_rows(coarse_image, share) + saturation - prolong_rows(previous_image, share)
        if parareal_no + 1 < PARAREAL:
            arrived_start = passed_along(ends, "tm", 1)
            starts = jnp.where(slice_index == 0, initial_rows, arrived_start)
        previous_image = coarse_image
    ends, pressure = from_rows(jnp.stack([ends, pressure]))
    return (ends[None], pressure[None])


def solution(mesh):
    in_specs = (
        P("sx", "sy", None),
        P("sx", "sy", None),
        P("sx", "sy", None),
        P("sx", "sy", None),
        P("sx", "sy", None),
        P(),
        P(),
    )
    out_specs = (P("tm", "sx", "sy", None), P("tm", "sx", "sy", None))
    return jax.shard_map(local, mesh=mesh, in_specs=in_specs, out_specs=out_specs, check_vma=False)
```

```python
import jax
import jax.numpy as jnp
from jax import lax
from jax.sharding import PartitionSpec as P

FSTEPS = 1
NEWTON = 2
CG_ITERS = 3
SWEEPS = 3
PARAREAL = 2
ROCKS = 4


mu_water = 1.0
mu_oil = 4.0
compress = 0.05
step_dt = 0.25
damping = 0.8


def extended(array, sides, width):
    for axis, dim in sides:
        size, length = (lax.axis_size(axis), array.shape[dim])
        up = [(i, (i + 1) % size) for i in range(size - 1)]
        down = [(j, i) for i, j in up]
        last = lax.slice_in_dim(array, length - width, length, axis=dim)
        initial = lax.slice_in_dim(array, 0, width, axis=dim)
        before = lax.ppermute(last, axis, up)
        after = lax.ppermute(initial, axis, down)
        array = jnp.concatenate([before, array, after], axis=dim)
    return array


def passed_along(value, axis, steps):
    count = lax.axis_size(axis)
    initial, last = (max(0, -steps), min(count, count - steps))
    return lax.ppermute(value, axis, [(source, source + steps) for source in range(initial, last)])


def lookup(rock_cells, end_values):
    summed_total = jnp.zeros(rock_cells.shape, end_values.dtype)
    for rock_kind in range(ROCKS):
        summed_total = summed_total + jnp.where(
            rock_cells == rock_kind, end_values[rock_kind], jnp.zeros((), end_values.dtype)
        )
    return summed_total


def restrict(volume):
    return volume.reshape(
        volume.shape[0] // 2, 2, volume.shape[1] // 2, 2, volume.shape[2] // 2, 2
    ).mean(axis=(1, 3, 5))


def prolong(volume):
    first, second, third = volume.shape
    spread_out = jnp.broadcast_to(
        volume[:, None, :, None, :, None], (first, 2, second, 2, third, 2)
    )
    return spread_out.reshape(2 * first, 2 * second, 2 * third)


def pad_depth(volume):
    return jnp.pad(volume, ((0, 0), (0, 0), (1, 1)))


def face_list(padded):
    return [
        padded[2:, 1:-1, 1:-1],
        padded[:-2, 1:-1, 1:-1],
        padded[1:-1, 2:, 1:-1],
        padded[1:-1, :-2, 1:-1],
        padded[1:-1, 1:-1, 2:],
        padded[1:-1, 1:-1, :-2],
    ]


ROW_AXES = ("sx", "sy")


def row_halo(volume):
    count = lax.axis_size("sx") * lax.axis_size("sy")
    up = [(i, i + 1) for i in range(count - 1)]
    down = [(i + 1, i) for i in range(count - 1)]
    before = lax.ppermute(volume[-1:], ROW_AXES, up)
    after = lax.ppermute(volume[:1], ROW_AXES, down)
    return jnp.concatenate([before, volume, after], axis=0)


def row_faces(volume):
    return face_list(jnp.pad(row_halo(volume), ((0, 0), (1, 1), (1, 1))))


def face_mobility_values(volume):
    return row_faces(volume)


def direction_spread(volume):
    return extended(volume, (("sx", 0), ("sy", 1)), 1)


def pressure_faces(volume):
    return row_faces(volume)


def flow_faces(volume):
    return row_faces(volume)


def build_face_tables(volume):
    return face_list(pad_depth(extended(volume, (("sx", 0), ("sy", 1)), 1)))


def coarse_faces(volume):
    return face_list(pad_depth(extended(volume, (("sx", 0), ("sy", 1)), 1)))


def accumulate_terms(summand_terms):
    summed_total = summand_terms[0]
    for summand_term in summand_terms[1:]:
        summed_total = summed_total + summand_term
    return summed_total


def mobilities(saturation, water_end, oil_end):
    water_mobility = water_end * saturation * saturation / mu_water
    oil_mobility = oil_end * (1.0 - saturation) * (1.0 - saturation) / mu_oil
    return (water_mobility, oil_mobility)


def fractional(saturation, water_end, oil_end):
    water_mobility, oil_mobility = mobilities(saturation, water_end, oil_end)
    mobility = water_mobility + oil_mobility
    water_slope = 2.0 * water_end * saturation / mu_water
    oil_slope = -2.0 * oil_end * (1.0 - saturation) / mu_oil
    return (
        water_mobility / mobility,
        (water_slope * oil_mobility - water_mobility * oil_slope) / (mobility * mobility),
    )


def upwind(frac, frac_beyond, outflows):
    return accumulate_terms(
        [
            jnp.maximum(outward, 0.0) * frac + jnp.minimum(outward, 0.0) * exceeding_part
            for outward, exceeding_part in zip(outflows, frac_beyond)
        ]
    )


def global_sums(values):
    count = lax.axis_size("sx") * lax.axis_size("sy")
    packed = jnp.broadcast_to(jnp.stack(values)[None], (count, len(values)))
    gathered = lax.all_to_all(packed, ("sx", "sy"), 0, 0, tiled=True)
    totals = jnp.sum(gathered, axis=0)
    return [totals[k] for k in range(len(values))]


def apply_operator(diagonal, transmissibility, vector):
    return diagonal * vector - accumulate_terms(
        [
            conduct_face * exceeding_part
            for conduct_face, exceeding_part in zip(transmissibility, row_faces(vector))
        ]
    )


def solve_pressure(source_rate, diagonal, transmissibility):
    residual = source_rate
    solution = None
    for sweep_no in range(CG_ITERS):
        precond = residual / diagonal
        image = apply_operator(diagonal, transmissibility, precond)
        rho_next, curvature = global_sums([jnp.sum(residual * precond), jnp.sum(precond * image)])
        if sweep_no == 0:
            step_len = rho_next / curvature
            direction = precond
            applied = image
            solution = step_len * direction
        else:
            ratio = rho_next / rho_now
            step_len = rho_next / (curvature - ratio * rho_next / step_len)
            direction = precond + ratio * direction
            applied = image + ratio * applied
            solution = solution + step_len * direction
        if sweep_no + 1 < CG_ITERS:
            residual = residual - step_len * applied
        rho_now = rho_next
    return solution


def fine_step(sat_old, permeability, porosity, source_rate, water_end, oil_end):
    water_mobility, oil_mobility = mobilities(sat_old, water_end, oil_end)
    transport_field = permeability * (water_mobility + oil_mobility)
    transmissibility = [
        0.5 * (transport_field + exceeding_part)
        for exceeding_part in face_mobility_values(transport_field)
    ]
    diagonal = compress + accumulate_terms(transmissibility)
    pressure = solve_pressure(source_rate, diagonal, transmissibility)
    beside = pressure_faces(pressure)
    outflows = [
        conduct_face * (pressure - exceeding_part)
        for conduct_face, exceeding_part in zip(transmissibility, beside)
    ]
    outgoing = accumulate_terms([jnp.maximum(outward, 0.0) for outward in outflows])
    saturation = sat_old
    for newton_no in range(NEWTON):
        frac, frac_slope = fractional(saturation, water_end, oil_end)
        flux_sum = upwind(frac, flow_faces(frac), outflows)
        balance = (
            porosity * (saturation - sat_old) / step_dt
            + flux_sum
            - jnp.maximum(source_rate, 0.0)
            - jnp.minimum(source_rate, 0.0) * frac
        )
        slope_sum = porosity / step_dt + jnp.abs(frac_slope) * (
            outgoing + jnp.maximum(-source_rate, 0.0)
        )
        saturation = saturation - balance / slope_sum
    return (saturation, pressure)


def gather_grid(blocks):
    rows, cols = (lax.axis_size("sx"), lax.axis_size("sy"))
    packed = jnp.broadcast_to(blocks[None], (rows * cols,) + blocks.shape)
    gathered = lax.all_to_all(packed, ("sx", "sy"), 0, 0, tiled=True)
    fields, depth_x, depth_y, depth_z = blocks.shape
    gathered = gathered.reshape(rows, cols, fields, depth_x, depth_y, depth_z)
    gathered = gathered.transpose(2, 0, 3, 1, 4, 5)
    return gathered.reshape(fields, rows * depth_x, cols * depth_y, depth_z)


def own_block(whole, shape):
    corner = (lax.axis_index("sx") * shape[0], lax.axis_index("sy") * shape[1], 0)
    return lax.dynamic_slice(whole, corner, shape)


def to_rows(blocks):
    columns = lax.axis_size("sy")
    fields, depth_x, depth_y, depth_z = blocks.shape
    share = depth_x // columns
    packed = blocks.reshape(fields, columns, share, depth_y, depth_z).transpose(1, 0, 2, 3, 4)
    got = lax.all_to_all(packed, "sy", 0, 0, tiled=True)
    return got.transpose(1, 2, 0, 3, 4).reshape(fields, share, columns * depth_y, depth_z)


def from_rows(rows):
    columns = lax.axis_size("sy")
    fields, share, length_y, depth_z = rows.shape
    depth_y = length_y // columns
    packed = rows.reshape(fields, share, columns, depth_y, depth_z).transpose(2, 0, 1, 3, 4)
    got = lax.all_to_all(packed, "sy", 0, 0, tiled=True)
    return got.transpose(1, 0, 2, 3, 4).reshape(fields, columns * share, depth_y, depth_z)


def row_index():
    return lax.axis_index("sx") * lax.axis_size("sy") + lax.axis_index("sy")


def restrict_rows(rows):
    share, length_y, depth_z = rows.shape
    partial = rows.reshape(share, length_y // 2, 2, depth_z // 2, 2).sum(axis=(2, 4))
    count = lax.axis_size("sx") * lax.axis_size("sy")
    packed = jnp.broadcast_to(partial[None], (count,) + partial.shape)
    gathered = lax.all_to_all(packed, ROW_AXES, 0, 0, tiled=True)
    gathered = gathered.reshape(count * share // 2, 2, length_y // 2, depth_z // 2)
    return gathered.sum(axis=1) / 8.0


def prolong_rows(whole, share):
    coarse_rows = (row_index() * share + jnp.arange(share)) // 2
    picked = jnp.take(whole, coarse_rows, axis=0)
    count, length_y, depth_z = picked.shape
    spread_out = jnp.broadcast_to(picked[:, :, None, :, None], (count, length_y, 2, depth_z, 2))
    return spread_out.reshape(count, 2 * length_y, 2 * depth_z)


def whole_faces(volume):
    return face_list(jnp.pad(volume, 1))


def local(
    initial_saturation, permeability, porosity, source_rate, rock_type, water_endpoint, oil_endpoint
):
    slices = lax.axis_size("tm")
    slice_index = lax.axis_index("tm")
    water_block = lookup(rock_type, water_endpoint)
    oil_block = lookup(rock_type, oil_endpoint)
    start_block = restrict(initial_saturation)
    block_shape = start_block.shape
    whole = gather_grid(
        jnp.stack(
            [
                start_block,
                restrict(permeability),
                restrict(porosity),
                restrict(source_rate),
                water_block,
                oil_block,
            ]
        )
    )
    start_coarse, permeability_upscaled, poro_coarse, source_coarse, water_coarse, oil_coarse = (
        whole[k] for k in range(6)
    )
    water_mobility, oil_mobility = mobilities(start_coarse, water_coarse, oil_coarse)
    transport_field_upscaled = permeability_upscaled * (water_mobility + oil_mobility)
    transmissibility_upscaled = [
        (transport_field_upscaled + exceeding_part) / 8.0
        for exceeding_part in whole_faces(transport_field_upscaled)
    ]
    diag_coarse = compress + accumulate_terms(transmissibility_upscaled)
    pressure_coarse = damping * source_coarse / diag_coarse
    for sweep_no in range(SWEEPS - 1):
        coupled = accumulate_terms(
            [
                conduct_face * exceeding_part
                for conduct_face, exceeding_part in zip(
                    transmissibility_upscaled, whole_faces(pressure_coarse)
                )
            ]
        )
        pressure_coarse = (
            pressure_coarse
            + damping * (source_coarse - (diag_coarse * pressure_coarse - coupled)) / diag_coarse
        )
    flows_coarse = [
        conduct_face * (pressure_coarse - exceeding_part)
        for conduct_face, exceeding_part in zip(transmissibility_upscaled, whole_faces(pressure_coarse))
    ]
    outgoing_coarse = accumulate_terms([jnp.maximum(outward, 0.0) for outward in flows_coarse])
    coarse_dt = FSTEPS * step_dt

    def coarse_step(coarse_state):
        frac, frac_slope = fractional(coarse_state, water_coarse, oil_coarse)
        flux_sum = upwind(frac, whole_faces(frac), flows_coarse)
        balance = (
            flux_sum - jnp.maximum(source_coarse, 0.0) - jnp.minimum(source_coarse, 0.0) * frac
        )
        slope_sum = poro_coarse / coarse_dt + jnp.abs(frac_slope) * (
            outgoing_coarse + jnp.maximum(-source_coarse, 0.0)
        )
        return coarse_state - balance / slope_sum

    def chain(corrections):

        def relay_round(turn_no, coarse_state):
            coarse_image = coarse_step(coarse_state)
            if corrections is None:
                outgoing_state = coarse_image
            else:
                outgoing_state = coarse_image + corrections
            arrived = passed_along(outgoing_state, "tm", 1)
            return jnp.where(slice_index == 0, start_coarse, arrived)

        coarse_state = lax.fori_loop(0, slices - 1, relay_round, start_coarse)
        return (coarse_state, coarse_step(coarse_state))

    initial_rows, permeability, porosity, source_rate, water_fine, oil_fine = to_rows(
        jnp.stack(
            [
                initial_saturation,
                permeability,
                porosity,
                source_rate,
                prolong(water_block),
                prolong(oil_block),
            ]
        )
    )
    share = initial_rows.shape[0]
    def own_chain(turn_no, carried):
        coarse_state, own_state, own_image = carried
        coarse_image = coarse_step(coarse_state)
        mine = turn_no == slice_index
        own_state = jnp.where(mine, coarse_state, own_state)
        own_image = jnp.where(mine, coarse_image, own_image)
        return (coarse_image, own_state, own_image)

    _, coarse_state, coarse_image = lax.fori_loop(
        0, slices, own_chain, (start_coarse, start_coarse, start_coarse)
    )
    starts = jnp.where(slice_index == 0, initial_rows, prolong_rows(coarse_state, share))
    previous_image = coarse_image
    ends = starts
    pressure = starts
    for parareal_no in range(PARAREAL):
        saturation = starts
        saturation, fine_pressure = fine_step(
            saturation, permeability, porosity, source_rate, water_fine, oil_fine
        )
        pressure = fine_pressure
        corrections = restrict_rows(saturation) - previous_image
        coarse_state, coarse_image = chain(corrections)
        ends = prolong_rows(coarse_image, share) + saturation - prolong_rows(previous_image, share)
        if parareal_no + 1 < PARAREAL:
            arrived_start = passed_along(ends, "tm", 1)
            starts = jnp.where(slice_index == 0, initial_rows, arrived_start)
        previous_image = coarse_image
    ends, pressure = from_rows(jnp.stack([ends, pressure]))
    return (ends[None], pressure[None])


def solution(mesh):
    in_specs = (
        P("sx", "sy", None),
        P("sx", "sy", None),
        P("sx", "sy", None),
        P("sx", "sy", None),
        P("sx", "sy", None),
        P(),
        P(),
    )
    out_specs = (P("tm", "sx", "sy", None), P("tm", "sx", "sy", None))
    return jax.shard_map(local, mesh=mesh, in_specs=in_specs, out_specs=out_specs, check_vma=False)
```

```python
import jax
import jax.numpy as jnp
from jax import lax
from jax.sharding import PartitionSpec as P

FSTEPS = 1
NEWTON = 2
CG_ITERS = 3
SWEEPS = 3
PARAREAL = 2
ROCKS = 4


mu_water = 1.0
mu_oil = 4.0
compress = 0.05
step_dt = 0.25
damping = 0.8


def extended(array, sides, width):
    for axis, dim in sides:
        size, length = (lax.axis_size(axis), array.shape[dim])
        up = [(i, (i + 1) % size) for i in range(size - 1)]
        down = [(j, i) for i, j in up]
        last = lax.slice_in_dim(array, length - width, length, axis=dim)
        initial = lax.slice_in_dim(array, 0, width, axis=dim)
        before = lax.ppermute(last, axis, up)
        after = lax.ppermute(initial, axis, down)
        array = jnp.concatenate([before, array, after], axis=dim)
    return array


def passed_along(value, axis, steps):
    count = lax.axis_size(axis)
    initial, last = (max(0, -steps), min(count, count - steps))
    return lax.ppermute(value, axis, [(source, source + steps) for source in range(initial, last)])


def lookup(rock_cells, end_values):
    summed_total = jnp.zeros(rock_cells.shape, end_values.dtype)
    for rock_kind in range(ROCKS):
        summed_total = summed_total + jnp.where(
            rock_cells == rock_kind, end_values[rock_kind], jnp.zeros((), end_values.dtype)
        )
    return summed_total


def restrict(volume):
    return volume.reshape(
        volume.shape[0] // 2, 2, volume.shape[1] // 2, 2, volume.shape[2] // 2, 2
    ).mean(axis=(1, 3, 5))


def prolong(volume):
    first, second, third = volume.shape
    spread_out = jnp.broadcast_to(
        volume[:, None, :, None, :, None], (first, 2, second, 2, third, 2)
    )
    return spread_out.reshape(2 * first, 2 * second, 2 * third)


def pad_depth(volume):
    return jnp.pad(volume, ((0, 0), (0, 0), (1, 1)))


def face_list(padded):
    return [
        padded[2:, 1:-1, 1:-1],
        padded[:-2, 1:-1, 1:-1],
        padded[1:-1, 2:, 1:-1],
        padded[1:-1, :-2, 1:-1],
        padded[1:-1, 1:-1, 2:],
        padded[1:-1, 1:-1, :-2],
    ]


ROW_AXES = ("sx", "sy")


def row_halo(volume):
    count = lax.axis_size("sx") * lax.axis_size("sy")
    up = [(i, i + 1) for i in range(count - 1)]
    down = [(i + 1, i) for i in range(count - 1)]
    before = lax.ppermute(volume[-1:], ROW_AXES, up)
    after = lax.ppermute(volume[:1], ROW_AXES, down)
    return jnp.concatenate([before, volume, after], axis=0)


def row_faces(volume):
    return face_list(jnp.pad(row_halo(volume), ((0, 0), (1, 1), (1, 1))))


def face_mobility_values(volume):
    return row_faces(volume)


def direction_spread(volume):
    return extended(volume, (("sx", 0), ("sy", 1)), 1)


def pressure_faces(volume):
    return row_faces(volume)


def flow_faces(volume):
    return row_faces(volume)


def build_face_tables(volume):
    return face_list(pad_depth(extended(volume, (("sx", 0), ("sy", 1)), 1)))


def coarse_faces(volume):
    return face_list(pad_depth(extended(volume, (("sx", 0), ("sy", 1)), 1)))


def accumulate_terms(summand_terms):
    summed_total = summand_terms[0]
    for summand_term in summand_terms[1:]:
        summed_total = summed_total + summand_term
    return summed_total


def mobilities(saturation, water_end, oil_end):
    water_mobility = water_end * saturation * saturation / mu_water
    oil_mobility = oil_end * (1.0 - saturation) * (1.0 - saturation) / mu_oil
    return (water_mobility, oil_mobility)


def fractional(saturation, water_end, oil_end):
    water_mobility, oil_mobility = mobilities(saturation, water_end, oil_end)
    mobility = water_mobility + oil_mobility
    water_slope = 2.0 * water_end * saturation / mu_water
    oil_slope = -2.0 * oil_end * (1.0 - saturation) / mu_oil
    return (
        water_mobility / mobility,
        (water_slope * oil_mobility - water_mobility * oil_slope) / (mobility * mobility),
    )


def upwind(frac, frac_beyond, outflows):
    return accumulate_terms(
        [
            jnp.maximum(outward, 0.0) * frac + jnp.minimum(outward, 0.0) * exceeding_part
            for outward, exceeding_part in zip(outflows, frac_beyond)
        ]
    )


def global_sums(values):
    count = lax.axis_size("sx") * lax.axis_size("sy")
    packed = jnp.broadcast_to(jnp.stack(values)[None], (count, len(values)))
    gathered = lax.all_to_all(packed, ("sx", "sy"), 0, 0, tiled=True)
    totals = jnp.sum(gathered, axis=0)
    return [totals[k] for k in range(len(values))]


def apply_operator(diagonal, transmissibility, vector):
    return diagonal * vector - accumulate_terms(
        [
            conduct_face * exceeding_part
            for conduct_face, exceeding_part in zip(transmissibility, row_faces(vector))
        ]
    )


def solve_pressure(source_rate, diagonal, transmissibility):
    residual = source_rate
    solution = None
    for sweep_no in range(CG_ITERS):
        precond = residual / diagonal
        image = apply_operator(diagonal, transmissibility, precond)
        rho_next, curvature = global_sums([jnp.sum(residual * precond), jnp.sum(precond * image)])
        if sweep_no == 0:
            step_len = rho_next / curvature
            direction = precond
            applied = image
            solution = step_len * direction
        else:
            ratio = rho_next / rho_now
            step_len = rho_next / (curvature - ratio * rho_next / step_len)
            direction = precond + ratio * direction
            applied = image + ratio * applied
            solution = solution + step_len * direction
        if sweep_no + 1 < CG_ITERS:
            residual = residual - step_len * applied
        rho_now = rho_next
    return solution


def fine_step(sat_old, permeability, porosity, source_rate, water_end, oil_end):
    water_mobility, oil_mobility = mobilities(sat_old, water_end, oil_end)
    transport_field = permeability * (water_mobility + oil_mobility)
    transmissibility = [
        0.5 * (transport_field + exceeding_part)
        for exceeding_part in face_mobility_values(transport_field)
    ]
    diagonal = compress + accumulate_terms(transmissibility)
    pressure = solve_pressure(source_rate, diagonal, transmissibility)
    beside = pressure_faces(pressure)
    outflows = [
        conduct_face * (pressure - exceeding_part)
        for conduct_face, exceeding_part in zip(transmissibility, beside)
    ]
    outgoing = accumulate_terms([jnp.maximum(outward, 0.0) for outward in outflows])
    saturation = sat_old
    for newton_no in range(NEWTON):
        frac, frac_slope = fractional(saturation, water_end, oil_end)
        flux_sum = upwind(frac, flow_faces(frac), outflows)
        balance = (
            porosity * (saturation - sat_old) / step_dt
            + flux_sum
            - jnp.maximum(source_rate, 0.0)
            - jnp.minimum(source_rate, 0.0) * frac
        )
        slope_sum = porosity / step_dt + jnp.abs(frac_slope) * (
            outgoing + jnp.maximum(-source_rate, 0.0)
        )
        saturation = saturation - balance / slope_sum
    return (saturation, pressure)


def gather_grid(blocks):
    rows, cols = (lax.axis_size("sx"), lax.axis_size("sy"))
    packed = jnp.broadcast_to(blocks[None], (rows * cols,) + blocks.shape)
    gathered = lax.all_to_all(packed, ("sx", "sy"), 0, 0, tiled=True)
    fields, depth_x, depth_y, depth_z = blocks.shape
    gathered = gathered.reshape(rows, cols, fields, depth_x, depth_y, depth_z)
    gathered = gathered.transpose(2, 0, 3, 1, 4, 5)
    return gathered.reshape(fields, rows * depth_x, cols * depth_y, depth_z)


def own_block(whole, shape):
    corner = (lax.axis_index("sx") * shape[0], lax.axis_index("sy") * shape[1], 0)
    return lax.dynamic_slice(whole, corner, shape)


def to_rows(blocks):
    columns = lax.axis_size("sy")
    fields, depth_x, depth_y, depth_z = blocks.shape
    share = depth_x // columns
    packed = blocks.reshape(fields, columns, share, depth_y, depth_z).transpose(1, 0, 2, 3, 4)
    got = lax.all_to_all(packed, "sy", 0, 0, tiled=True)
    return got.transpose(1, 2, 0, 3, 4).reshape(fields, share, columns * depth_y, depth_z)


def from_rows(rows):
    columns = lax.axis_size("sy")
    fields, share, length_y, depth_z = rows.shape
    depth_y = length_y // columns
    packed = rows.reshape(fields, share, columns, depth_y, depth_z).transpose(2, 0, 1, 3, 4)
    got = lax.all_to_all(packed, "sy", 0, 0, tiled=True)
    return got.transpose(1, 0, 2, 3, 4).reshape(fields, columns * share, depth_y, depth_z)


def row_index():
    return lax.axis_index("sx") * lax.axis_size("sy") + lax.axis_index("sy")


def restrict_rows(rows):
    share, length_y, depth_z = rows.shape
    partial = rows.reshape(share, length_y // 2, 2, depth_z // 2, 2).sum(axis=(2, 4))
    count = lax.axis_size("sx") * lax.axis_size("sy")
    packed = jnp.broadcast_to(partial[None], (count,) + partial.shape)
    gathered = lax.all_to_all(packed, ROW_AXES, 0, 0, tiled=True)
    gathered = gathered.reshape(count * share // 2, 2, length_y // 2, depth_z // 2)
    return gathered.sum(axis=1) / 8.0


def prolong_rows(whole, share):
    coarse_rows = (row_index() * share + jnp.arange(share)) // 2
    picked = jnp.take(whole, coarse_rows, axis=0)
    count, length_y, depth_z = picked.shape
    spread_out = jnp.broadcast_to(picked[:, :, None, :, None], (count, length_y, 2, depth_z, 2))
    return spread_out.reshape(count, 2 * length_y, 2 * depth_z)


def whole_faces(volume):
    return face_list(jnp.pad(volume, 1))


def local(
    initial_saturation, permeability, porosity, source_rate, rock_type, water_endpoint, oil_endpoint
):
    slices = lax.axis_size("tm")
    slice_index = lax.axis_index("tm")
    water_block = lookup(rock_type, water_endpoint)
    oil_block = lookup(rock_type, oil_endpoint)
    start_block = restrict(initial_saturation)
    block_shape = start_block.shape
    whole = gather_grid(
        jnp.stack(
            [
                start_block,
                restrict(permeability),
                restrict(porosity),
                restrict(source_rate),
                water_block,
                oil_block,
            ]
        )
    )
    start_coarse, permeability_upscaled, poro_coarse, source_coarse, water_coarse, oil_coarse = (
        whole[k] for k in range(6)
    )
    water_mobility, oil_mobility = mobilities(start_coarse, water_coarse, oil_coarse)
    transport_field_upscaled = permeability_upscaled * (water_mobility + oil_mobility)
    transmissibility_upscaled = [
        (transport_field_upscaled + exceeding_part) / 8.0
        for exceeding_part in whole_faces(transport_field_upscaled)
    ]
    diag_coarse = compress + accumulate_terms(transmissibility_upscaled)
    pressure_coarse = damping * source_coarse / diag_coarse
    for sweep_no in range(SWEEPS - 1):
        coupled = accumulate_terms(
            [
                conduct_face * exceeding_part
                for conduct_face, exceeding_part in zip(
                    transmissibility_upscaled, whole_faces(pressure_coarse)
                )
            ]
        )
        pressure_coarse = (
            pressure_coarse
            + damping * (source_coarse - (diag_coarse * pressure_coarse - coupled)) / diag_coarse
        )
    flows_coarse = [
        conduct_face * (pressure_coarse - exceeding_part)
        for conduct_face, exceeding_part in zip(transmissibility_upscaled, whole_faces(pressure_coarse))
    ]
    outgoing_coarse = accumulate_terms([jnp.maximum(outward, 0.0) for outward in flows_coarse])
    coarse_dt = FSTEPS * step_dt

    def coarse_step(coarse_state):
        frac, frac_slope = fractional(coarse_state, water_coarse, oil_coarse)
        flux_sum = upwind(frac, whole_faces(frac), flows_coarse)
        balance = (
            flux_sum - jnp.maximum(source_coarse, 0.0) - jnp.minimum(source_coarse, 0.0) * frac
        )
        slope_sum = poro_coarse / coarse_dt + jnp.abs(frac_slope) * (
            outgoing_coarse + jnp.maximum(-source_coarse, 0.0)
        )
        return coarse_state - balance / slope_sum

    def chain(corrections):

        def relay_round(turn_no, arrived):
            coarse_state = jnp.where(slice_index == 0, start_coarse, arrived)
            return passed_along(coarse_step(coarse_state) + corrections, "tm", 1)

        arrived = lax.fori_loop(0, slices - 1, relay_round, start_coarse)
        coarse_state = jnp.where(slice_index == 0, start_coarse, arrived)
        return (coarse_state, coarse_step(coarse_state))

    coarse_state = lax.fori_loop(
        0, slice_index, lambda turn_no, state: coarse_step(state), start_coarse
    )
    coarse_image = coarse_step(coarse_state)
    initial_rows, permeability, porosity, source_rate, water_fine, oil_fine = to_rows(
        jnp.stack(
            [
                initial_saturation,
                permeability,
                porosity,
                source_rate,
                prolong(water_block),
                prolong(oil_block),
            ]
        )
    )
    share = initial_rows.shape[0]
    def own_chain(turn_no, carried):
        coarse_state, own_state, own_image = carried
        coarse_image = coarse_step(coarse_state)
        mine = turn_no == slice_index
        own_state = jnp.where(mine, coarse_state, own_state)
        own_image = jnp.where(mine, coarse_image, own_image)
        return (coarse_image, own_state, own_image)

    _, coarse_state, coarse_image = lax.fori_loop(
        0, slices, own_chain, (start_coarse, start_coarse, start_coarse)
    )
    starts = jnp.where(slice_index == 0, initial_rows, prolong_rows(coarse_state, share))
    previous_image = coarse_image
    ends = starts
    pressure = starts
    for parareal_no in range(PARAREAL):
        saturation = starts
        saturation, fine_pressure = fine_step(
            saturation, permeability, porosity, source_rate, water_fine, oil_fine
        )
        pressure = fine_pressure
        corrections = restrict_rows(saturation) - previous_image
        coarse_state, coarse_image = chain(corrections)
        ends = prolong_rows(coarse_image, share) + saturation - prolong_rows(previous_image, share)
        if parareal_no + 1 < PARAREAL:
            arrived_start = passed_along(ends, "tm", 1)
            starts = jnp.where(slice_index == 0, initial_rows, arrived_start)
        previous_image = coarse_image
    ends, pressure = from_rows(jnp.stack([ends, pressure]))
    return (ends[None], pressure[None])


def solution(mesh):
    in_specs = (
        P("sx", "sy", None),
        P("sx", "sy", None),
        P("sx", "sy", None),
        P("sx", "sy", None),
        P("sx", "sy", None),
        P(),
        P(),
    )
    out_specs = (P("tm", "sx", "sy", None), P("tm", "sx", "sy", None))
    return jax.shard_map(local, mesh=mesh, in_specs=in_specs, out_specs=out_specs, check_vma=False)
```

```python
import jax
import jax.numpy as jnp
from jax import lax
from jax.sharding import PartitionSpec as P

FSTEPS = 1
NEWTON = 2
CG_ITERS = 3
SWEEPS = 3
PARAREAL = 2
ROCKS = 4


mu_water = 1.0
mu_oil = 4.0
compress = 0.05
step_dt = 0.25
damping = 0.8


def extended(array, sides, width):
    for axis, dim in sides:
        size, length = (lax.axis_size(axis), array.shape[dim])
        up = [(i, (i + 1) % size) for i in range(size - 1)]
        down = [(j, i) for i, j in up]
        last = lax.slice_in_dim(array, length - width, length, axis=dim)
        initial = lax.slice_in_dim(array, 0, width, axis=dim)
        before = lax.ppermute(last, axis, up)
        after = lax.ppermute(initial, axis, down)
        array = jnp.concatenate([before, array, after], axis=dim)
    return array


def passed_along(value, axis, steps):
    count = lax.axis_size(axis)
    initial, last = (max(0, -steps), min(count, count - steps))
    return lax.ppermute(value, axis, [(source, source + steps) for source in range(initial, last)])


def lookup(rock_cells, end_values):
    summed_total = jnp.zeros(rock_cells.shape, end_values.dtype)
    for rock_kind in range(ROCKS):
        summed_total = summed_total + jnp.where(
            rock_cells == rock_kind, end_values[rock_kind], jnp.zeros((), end_values.dtype)
        )
    return summed_total


def restrict(volume):
    return volume.reshape(
        volume.shape[0] // 2, 2, volume.shape[1] // 2, 2, volume.shape[2] // 2, 2
    ).mean(axis=(1, 3, 5))


def prolong(volume):
    first, second, third = volume.shape
    spread_out = jnp.broadcast_to(
        volume[:, None, :, None, :, None], (first, 2, second, 2, third, 2)
    )
    return spread_out.reshape(2 * first, 2 * second, 2 * third)


def pad_depth(volume):
    return jnp.pad(volume, ((0, 0), (0, 0), (1, 1)))


def face_list(padded):
    return [
        padded[2:, 1:-1, 1:-1],
        padded[:-2, 1:-1, 1:-1],
        padded[1:-1, 2:, 1:-1],
        padded[1:-1, :-2, 1:-1],
        padded[1:-1, 1:-1, 2:],
        padded[1:-1, 1:-1, :-2],
    ]


ROW_AXES = ("sx", "sy")


def row_halo(volume):
    count = lax.axis_size("sx") * lax.axis_size("sy")
    up = [(i, i + 1) for i in range(count - 1)]
    down = [(i + 1, i) for i in range(count - 1)]
    before = lax.ppermute(volume[-1:], ROW_AXES, up)
    after = lax.ppermute(volume[:1], ROW_AXES, down)
    return jnp.concatenate([before, volume, after], axis=0)


def row_faces(volume):
    return face_list(jnp.pad(row_halo(volume), ((0, 0), (1, 1), (1, 1))))


def face_mobility_values(volume):
    return row_faces(volume)


def direction_spread(volume):
    return extended(volume, (("sx", 0), ("sy", 1)), 1)


def pressure_faces(volume):
    return row_faces(volume)


def flow_faces(volume):
    return row_faces(volume)


def build_face_tables(volume):
    return face_list(pad_depth(extended(volume, (("sx", 0), ("sy", 1)), 1)))


def coarse_faces(volume):
    return face_list(pad_depth(extended(volume, (("sx", 0), ("sy", 1)), 1)))


def accumulate_terms(summand_terms):
    summed_total = summand_terms[0]
    for summand_term in summand_terms[1:]:
        summed_total = summed_total + summand_term
    return summed_total


def mobilities(saturation, water_end, oil_end):
    water_mobility = water_end * saturation * saturation / mu_water
    oil_mobility = oil_end * (1.0 - saturation) * (1.0 - saturation) / mu_oil
    return (water_mobility, oil_mobility)


def fractional(saturation, water_end, oil_end):
    water_mobility, oil_mobility = mobilities(saturation, water_end, oil_end)
    mobility = water_mobility + oil_mobility
    water_slope = 2.0 * water_end * saturation / mu_water
    oil_slope = -2.0 * oil_end * (1.0 - saturation) / mu_oil
    return (
        water_mobility / mobility,
        (water_slope * oil_mobility - water_mobility * oil_slope) / (mobility * mobility),
    )


def upwind(frac, frac_beyond, outflows):
    return accumulate_terms(
        [
            jnp.maximum(outward, 0.0) * frac + jnp.minimum(outward, 0.0) * exceeding_part
            for outward, exceeding_part in zip(outflows, frac_beyond)
        ]
    )


def global_sums(values):
    count = lax.axis_size("sx") * lax.axis_size("sy")
    packed = jnp.broadcast_to(jnp.stack(values)[None], (count, len(values)))
    gathered = lax.all_to_all(packed, ("sx", "sy"), 0, 0, tiled=True)
    totals = jnp.sum(gathered, axis=0)
    return [totals[k] for k in range(len(values))]


def apply_operator(diagonal, transmissibility, vector):
    return diagonal * vector - accumulate_terms(
        [
            conduct_face * exceeding_part
            for conduct_face, exceeding_part in zip(transmissibility, row_faces(vector))
        ]
    )


def solve_pressure(source_rate, diagonal, transmissibility):
    residual = source_rate
    solution = None
    for sweep_no in range(CG_ITERS):
        precond = residual / diagonal
        image = apply_operator(diagonal, transmissibility, precond)
        rho_next, curvature = global_sums([jnp.sum(residual * precond), jnp.sum(precond * image)])
        if sweep_no == 0:
            step_len = rho_next / curvature
            direction = precond
            applied = image
            solution = step_len * direction
        else:
            ratio = rho_next / rho_now
            step_len = rho_next / (curvature - ratio * rho_next / step_len)
            direction = precond + ratio * direction
            applied = image + ratio * applied
            solution = solution + step_len * direction
        if sweep_no + 1 < CG_ITERS:
            residual = residual - step_len * applied
        rho_now = rho_next
    return solution


def fine_step(sat_old, permeability, porosity, source_rate, water_end, oil_end):
    water_mobility, oil_mobility = mobilities(sat_old, water_end, oil_end)
    transport_field = permeability * (water_mobility + oil_mobility)
    transmissibility = [
        0.5 * (transport_field + exceeding_part)
        for exceeding_part in face_mobility_values(transport_field)
    ]
    diagonal = compress + accumulate_terms(transmissibility)
    pressure = solve_pressure(source_rate, diagonal, transmissibility)
    beside = pressure_faces(pressure)
    outflows = [
        conduct_face * (pressure - exceeding_part)
        for conduct_face, exceeding_part in zip(transmissibility, beside)
    ]
    outgoing = accumulate_terms([jnp.maximum(outward, 0.0) for outward in outflows])
    saturation = sat_old
    for newton_no in range(NEWTON):
        frac, frac_slope = fractional(saturation, water_end, oil_end)
        flux_sum = upwind(frac, flow_faces(frac), outflows)
        balance = (
            porosity * (saturation - sat_old) / step_dt
            + flux_sum
            - jnp.maximum(source_rate, 0.0)
            - jnp.minimum(source_rate, 0.0) * frac
        )
        slope_sum = porosity / step_dt + jnp.abs(frac_slope) * (
            outgoing + jnp.maximum(-source_rate, 0.0)
        )
        saturation = saturation - balance / slope_sum
    return (saturation, pressure)


def gather_grid(blocks):
    rows, cols = (lax.axis_size("sx"), lax.axis_size("sy"))
    packed = jnp.broadcast_to(blocks[None], (rows * cols,) + blocks.shape)
    gathered = lax.all_to_all(packed, ("sx", "sy"), 0, 0, tiled=True)
    fields, depth_x, depth_y, depth_z = blocks.shape
    gathered = gathered.reshape(rows, cols, fields, depth_x, depth_y, depth_z)
    gathered = gathered.transpose(2, 0, 3, 1, 4, 5)
    return gathered.reshape(fields, rows * depth_x, cols * depth_y, depth_z)


def own_block(whole, shape):
    corner = (lax.axis_index("sx") * shape[0], lax.axis_index("sy") * shape[1], 0)
    return lax.dynamic_slice(whole, corner, shape)


def to_rows(blocks):
    columns = lax.axis_size("sy")
    fields, depth_x, depth_y, depth_z = blocks.shape
    share = depth_x // columns
    packed = blocks.reshape(fields, columns, share, depth_y, depth_z).transpose(1, 0, 2, 3, 4)
    got = lax.all_to_all(packed, "sy", 0, 0, tiled=True)
    return got.transpose(1, 2, 0, 3, 4).reshape(fields, share, columns * depth_y, depth_z)


def from_rows(rows):
    columns = lax.axis_size("sy")
    fields, share, length_y, depth_z = rows.shape
    depth_y = length_y // columns
    packed = rows.reshape(fields, share, columns, depth_y, depth_z).transpose(2, 0, 1, 3, 4)
    got = lax.all_to_all(packed, "sy", 0, 0, tiled=True)
    return got.transpose(1, 0, 2, 3, 4).reshape(fields, columns * share, depth_y, depth_z)


def row_index():
    return lax.axis_index("sx") * lax.axis_size("sy") + lax.axis_index("sy")


def restrict_rows(rows):
    share, length_y, depth_z = rows.shape
    partial = rows.reshape(share, length_y // 2, 2, depth_z // 2, 2).sum(axis=(2, 4))
    count = lax.axis_size("sx") * lax.axis_size("sy")
    packed = jnp.broadcast_to(partial[None], (count,) + partial.shape)
    gathered = lax.all_to_all(packed, ROW_AXES, 0, 0, tiled=True)
    gathered = gathered.reshape(count * share // 2, 2, length_y // 2, depth_z // 2)
    return gathered.sum(axis=1) / 8.0


def prolong_rows(whole, share):
    coarse_rows = (row_index() * share + jnp.arange(share)) // 2
    picked = jnp.take(whole, coarse_rows, axis=0)
    count, length_y, depth_z = picked.shape
    spread_out = jnp.broadcast_to(picked[:, :, None, :, None], (count, length_y, 2, depth_z, 2))
    return spread_out.reshape(count, 2 * length_y, 2 * depth_z)


def whole_faces(volume):
    return face_list(jnp.pad(volume, 1))


def local(
    initial_saturation, permeability, porosity, source_rate, rock_type, water_endpoint, oil_endpoint
):
    slices = lax.axis_size("tm")
    slice_index = lax.axis_index("tm")
    water_block = lookup(rock_type, water_endpoint)
    oil_block = lookup(rock_type, oil_endpoint)
    start_block = restrict(initial_saturation)
    block_shape = start_block.shape
    whole = gather_grid(
        jnp.stack(
            [
                start_block,
                restrict(permeability),
                restrict(porosity),
                restrict(source_rate),
                water_block,
                oil_block,
            ]
        )
    )
    start_coarse, permeability_upscaled, poro_coarse, source_coarse, water_coarse, oil_coarse = (
        whole[k] for k in range(6)
    )
    water_mobility, oil_mobility = mobilities(start_coarse, water_coarse, oil_coarse)
    transport_field_upscaled = permeability_upscaled * (water_mobility + oil_mobility)
    transmissibility_upscaled = [
        (transport_field_upscaled + exceeding_part) / 8.0
        for exceeding_part in whole_faces(transport_field_upscaled)
    ]
    diag_coarse = compress + accumulate_terms(transmissibility_upscaled)
    pressure_coarse = damping * source_coarse / diag_coarse
    for sweep_no in range(SWEEPS - 1):
        coupled = accumulate_terms(
            [
                conduct_face * exceeding_part
                for conduct_face, exceeding_part in zip(
                    transmissibility_upscaled, whole_faces(pressure_coarse)
                )
            ]
        )
        pressure_coarse = (
            pressure_coarse
            + damping * (source_coarse - (diag_coarse * pressure_coarse - coupled)) / diag_coarse
        )
    flows_coarse = [
        conduct_face * (pressure_coarse - exceeding_part)
        for conduct_face, exceeding_part in zip(transmissibility_upscaled, whole_faces(pressure_coarse))
    ]
    outgoing_coarse = accumulate_terms([jnp.maximum(outward, 0.0) for outward in flows_coarse])
    coarse_dt = FSTEPS * step_dt

    def coarse_step(coarse_state):
        frac, frac_slope = fractional(coarse_state, water_coarse, oil_coarse)
        flux_sum = upwind(frac, whole_faces(frac), flows_coarse)
        balance = (
            flux_sum - jnp.maximum(source_coarse, 0.0) - jnp.minimum(source_coarse, 0.0) * frac
        )
        slope_sum = poro_coarse / coarse_dt + jnp.abs(frac_slope) * (
            outgoing_coarse + jnp.maximum(-source_coarse, 0.0)
        )
        return coarse_state - balance / slope_sum

    def chain(corrections):

        def relay_round(turn_no, arrived):
            coarse_state = jnp.where(slice_index == 0, start_coarse, arrived)
            return passed_along(coarse_step(coarse_state) + corrections, "tm", 1)

        arrived = lax.fori_loop(0, slices - 1, relay_round, start_coarse)
        coarse_state = jnp.where(slice_index == 0, start_coarse, arrived)
        return (coarse_state, coarse_step(coarse_state))

    coarse_state = lax.fori_loop(
        0, slice_index, lambda turn_no, state: coarse_step(state), start_coarse
    )
    coarse_image = coarse_step(coarse_state)
    initial_rows, permeability, porosity, source_rate, water_fine, oil_fine = to_rows(
        jnp.stack(
            [
                initial_saturation,
                permeability,
                porosity,
                source_rate,
                prolong(water_block),
                prolong(oil_block),
            ]
        )
    )
    share = initial_rows.shape[0]
    starts = jnp.where(slice_index == 0, initial_rows, prolong_rows(coarse_state, share))
    previous_image = coarse_image
    ends = starts
    pressure = starts
    for parareal_no in range(PARAREAL):
        saturation = starts
        saturation, fine_pressure = fine_step(
            saturation, permeability, porosity, source_rate, water_fine, oil_fine
        )
        pressure = fine_pressure
        corrections = restrict_rows(saturation) - previous_image
        coarse_state, coarse_image = chain(corrections)
        ends = prolong_rows(coarse_image, share) + saturation - prolong_rows(previous_image, share)
        if parareal_no + 1 < PARAREAL:
            arrived_start = passed_along(ends, "tm", 1)
            starts = jnp.where(slice_index == 0, initial_rows, arrived_start)
        previous_image = coarse_image
    ends, pressure = from_rows(jnp.stack([ends, pressure]))
    return (ends[None], pressure[None])


def solution(mesh):
    in_specs = (
        P("sx", "sy", None),
        P("sx", "sy", None),
        P("sx", "sy", None),
        P("sx", "sy", None),
        P("sx", "sy", None),
        P(),
        P(),
    )
    out_specs = (P("tm", "sx", "sy", None), P("tm", "sx", "sy", None))
    return jax.shard_map(local, mesh=mesh, in_specs=in_specs, out_specs=out_specs, check_vma=False)
```

```python
import jax
import jax.numpy as jnp
from jax import lax
from jax.sharding import PartitionSpec as P

FSTEPS = 1
NEWTON = 2
CG_ITERS = 3
SWEEPS = 3
PARAREAL = 2
ROCKS = 4


mu_water = 1.0
mu_oil = 4.0
compress = 0.05
step_dt = 0.25
damping = 0.8


def extended(array, sides, width):
    for axis, dim in sides:
        size, length = (lax.axis_size(axis), array.shape[dim])
        up = [(i, (i + 1) % size) for i in range(size - 1)]
        down = [(j, i) for i, j in up]
        last = lax.slice_in_dim(array, length - width, length, axis=dim)
        initial = lax.slice_in_dim(array, 0, width, axis=dim)
        before = lax.ppermute(last, axis, up)
        after = lax.ppermute(initial, axis, down)
        array = jnp.concatenate([before, array, after], axis=dim)
    return array


def passed_along(value, axis, steps):
    count = lax.axis_size(axis)
    initial, last = (max(0, -steps), min(count, count - steps))
    return lax.ppermute(value, axis, [(source, source + steps) for source in range(initial, last)])


def lookup(rock_cells, end_values):
    summed_total = jnp.zeros(rock_cells.shape, end_values.dtype)
    for rock_kind in range(ROCKS):
        summed_total = summed_total + jnp.where(
            rock_cells == rock_kind, end_values[rock_kind], jnp.zeros((), end_values.dtype)
        )
    return summed_total


def restrict(volume):
    return volume.reshape(
        volume.shape[0] // 2, 2, volume.shape[1] // 2, 2, volume.shape[2] // 2, 2
    ).mean(axis=(1, 3, 5))


def prolong(volume):
    first, second, third = volume.shape
    spread_out = jnp.broadcast_to(
        volume[:, None, :, None, :, None], (first, 2, second, 2, third, 2)
    )
    return spread_out.reshape(2 * first, 2 * second, 2 * third)


def pair_matrix(count):
    rows = lax.broadcasted_iota(jnp.int32, (count, 2 * count), 0)
    cols = lax.broadcasted_iota(jnp.int32, (count, 2 * count), 1)
    return (cols // 2 == rows).astype(jnp.float32)


def sum_pairs_yz(volume):
    length_y, depth_z = volume.shape[-2:]
    lead = volume.shape[:-2]
    flat = volume.reshape((-1, length_y, depth_z))
    half_z = jnp.einsum("bkz,wz->bkw", flat, pair_matrix(depth_z // 2), precision=lax.Precision.HIGHEST)
    half_y = jnp.einsum("yk,bkw->byw", pair_matrix(length_y // 2), half_z, precision=lax.Precision.HIGHEST)
    return half_y.reshape(lead + (length_y // 2, depth_z // 2))


def spread_yz(volume):
    length_y, depth_z = volume.shape[-2:]
    lead = volume.shape[:-2]
    flat = volume.reshape((-1, length_y, depth_z))
    wide_z = jnp.einsum("bkz,zw->bkw", flat, pair_matrix(depth_z), precision=lax.Precision.HIGHEST)
    wide_y = jnp.einsum("ky,bkw->byw", pair_matrix(length_y), wide_z, precision=lax.Precision.HIGHEST)
    return wide_y.reshape(lead + (2 * length_y, 2 * depth_z))


def restrict_blocks(volume):
    fields, length_x, length_y, depth_z = volume.shape
    paired_x = volume.reshape(fields, length_x // 2, 2, length_y, depth_z).sum(axis=2)
    return sum_pairs_yz(paired_x) / 8.0


def prolong_blocks(volume):
    fields, length_x, length_y, depth_z = volume.shape
    spread = spread_yz(volume)
    spread = jnp.broadcast_to(spread[:, :, None], (fields, length_x, 2) + spread.shape[2:])
    return spread.reshape((fields, 2 * length_x) + spread.shape[3:])


def pad_depth(volume):
    return jnp.pad(volume, ((0, 0), (0, 0), (1, 1)))


def face_list(padded):
    return [
        padded[2:, 1:-1, 1:-1],
        padded[:-2, 1:-1, 1:-1],
        padded[1:-1, 2:, 1:-1],
        padded[1:-1, :-2, 1:-1],
        padded[1:-1, 1:-1, 2:],
        padded[1:-1, 1:-1, :-2],
    ]


ROW_AXES = ("sx", "sy")


def row_halo(volume):
    count = lax.axis_size("sx") * lax.axis_size("sy")
    up = [(i, i + 1) for i in range(count - 1)]
    down = [(i + 1, i) for i in range(count - 1)]
    before = lax.ppermute(volume[-1:], ROW_AXES, up)
    after = lax.ppermute(volume[:1], ROW_AXES, down)
    return jnp.concatenate([before, volume, after], axis=0)


def row_faces(volume):
    return face_list(jnp.pad(row_halo(volume), ((0, 0), (1, 1), (1, 1))))


def face_mobility_values(volume):
    return row_faces(volume)


def direction_spread(volume):
    return extended(volume, (("sx", 0), ("sy", 1)), 1)


def pressure_faces(volume):
    return row_faces(volume)


def flow_faces(volume):
    return row_faces(volume)


def build_face_tables(volume):
    return face_list(pad_depth(extended(volume, (("sx", 0), ("sy", 1)), 1)))


def coarse_faces(volume):
    return face_list(pad_depth(extended(volume, (("sx", 0), ("sy", 1)), 1)))


def accumulate_terms(summand_terms):
    summed_total = summand_terms[0]
    for summand_term in summand_terms[1:]:
        summed_total = summed_total + summand_term
    return summed_total


def mobilities(saturation, water_end, oil_end):
    water_mobility = water_end * saturation * saturation / mu_water
    oil_mobility = oil_end * (1.0 - saturation) * (1.0 - saturation) / mu_oil
    return (water_mobility, oil_mobility)


def fractional(saturation, water_end, oil_end):
    water_mobility, oil_mobility = mobilities(saturation, water_end, oil_end)
    mobility = water_mobility + oil_mobility
    water_slope = 2.0 * water_end * saturation / mu_water
    oil_slope = -2.0 * oil_end * (1.0 - saturation) / mu_oil
    return (
        water_mobility / mobility,
        (water_slope * oil_mobility - water_mobility * oil_slope) / (mobility * mobility),
    )


def upwind(frac, frac_beyond, outflows):
    return accumulate_terms(
        [
            jnp.maximum(outward, 0.0) * frac + jnp.minimum(outward, 0.0) * exceeding_part
            for outward, exceeding_part in zip(outflows, frac_beyond)
        ]
    )


def global_sums(values):
    count = lax.axis_size("sx") * lax.axis_size("sy")
    packed = jnp.broadcast_to(jnp.stack(values)[None], (count, len(values)))
    gathered = lax.all_to_all(packed, ("sx", "sy"), 0, 0, tiled=True)
    totals = jnp.sum(gathered, axis=0)
    return [totals[k] for k in range(len(values))]


def apply_operator(diagonal, transmissibility, vector):
    return diagonal * vector - accumulate_terms(
        [
            conduct_face * exceeding_part
            for conduct_face, exceeding_part in zip(transmissibility, row_faces(vector))
        ]
    )


def solve_pressure(source_rate, diagonal, transmissibility):
    residual = source_rate
    solution = None
    for sweep_no in range(CG_ITERS):
        precond = residual / diagonal
        image = apply_operator(diagonal, transmissibility, precond)
        rho_next, curvature = global_sums([jnp.sum(residual * precond), jnp.sum(precond * image)])
        if sweep_no == 0:
            step_len = rho_next / curvature
            direction = precond
            applied = image
            solution = step_len * direction
        else:
            ratio = rho_next / rho_now
            step_len = rho_next / (curvature - ratio * rho_next / step_len)
            direction = precond + ratio * direction
            applied = image + ratio * applied
            solution = solution + step_len * direction
        if sweep_no + 1 < CG_ITERS:
            residual = residual - step_len * applied
        rho_now = rho_next
    return solution


def fine_step(sat_old, permeability, porosity, source_rate, water_end, oil_end):
    water_mobility, oil_mobility = mobilities(sat_old, water_end, oil_end)
    transport_field = permeability * (water_mobility + oil_mobility)
    transmissibility = [
        0.5 * (transport_field + exceeding_part)
        for exceeding_part in face_mobility_values(transport_field)
    ]
    diagonal = compress + accumulate_terms(transmissibility)
    pressure = solve_pressure(source_rate, diagonal, transmissibility)
    beside = pressure_faces(pressure)
    outflows = [
        conduct_face * (pressure - exceeding_part)
        for conduct_face, exceeding_part in zip(transmissibility, beside)
    ]
    outgoing = accumulate_terms([jnp.maximum(outward, 0.0) for outward in outflows])
    saturation = sat_old
    for newton_no in range(NEWTON):
        frac, frac_slope = fractional(saturation, water_end, oil_end)
        flux_sum = upwind(frac, flow_faces(frac), outflows)
        balance = (
            porosity * (saturation - sat_old) / step_dt
            + flux_sum
            - jnp.maximum(source_rate, 0.0)
            - jnp.minimum(source_rate, 0.0) * frac
        )
        slope_sum = porosity / step_dt + jnp.abs(frac_slope) * (
            outgoing + jnp.maximum(-source_rate, 0.0)
        )
        saturation = saturation - balance / slope_sum
    return (saturation, pressure)


def gather_grid(blocks):
    rows, cols = (lax.axis_size("sx"), lax.axis_size("sy"))
    packed = jnp.broadcast_to(blocks[None], (rows * cols,) + blocks.shape)
    gathered = lax.all_to_all(packed, ("sx", "sy"), 0, 0, tiled=True)
    fields, depth_x, depth_y, depth_z = blocks.shape
    gathered = gathered.reshape(rows, cols, fields, depth_x, depth_y, depth_z)
    gathered = gathered.transpose(2, 0, 3, 1, 4, 5)
    return gathered.reshape(fields, rows * depth_x, cols * depth_y, depth_z)


def own_block(whole, shape):
    corner = (lax.axis_index("sx") * shape[0], lax.axis_index("sy") * shape[1], 0)
    return lax.dynamic_slice(whole, corner, shape)


def to_rows(blocks):
    columns = lax.axis_size("sy")
    fields, depth_x, depth_y, depth_z = blocks.shape
    share = depth_x // columns
    packed = blocks.reshape(fields, columns, share, depth_y, depth_z).transpose(1, 0, 2, 3, 4)
    got = lax.all_to_all(packed, "sy", 0, 0, tiled=True)
    return got.transpose(1, 2, 0, 3, 4).reshape(fields, share, columns * depth_y, depth_z)


def from_rows(rows):
    columns = lax.axis_size("sy")
    fields, share, length_y, depth_z = rows.shape
    depth_y = length_y // columns
    packed = rows.reshape(fields, share, columns, depth_y, depth_z).transpose(2, 0, 1, 3, 4)
    got = lax.all_to_all(packed, "sy", 0, 0, tiled=True)
    return got.transpose(1, 0, 2, 3, 4).reshape(fields, columns * share, depth_y, depth_z)


def row_index():
    return lax.axis_index("sx") * lax.axis_size("sy") + lax.axis_index("sy")


def restrict_rows(rows):
    share, length_y, depth_z = rows.shape
    partial = sum_pairs_yz(rows)
    count = lax.axis_size("sx") * lax.axis_size("sy")
    packed = jnp.broadcast_to(partial[None], (count,) + partial.shape)
    gathered = lax.all_to_all(packed, ROW_AXES, 0, 0, tiled=True)
    gathered = gathered.reshape(count * share // 2, 2, length_y // 2, depth_z // 2)
    return gathered.sum(axis=1) / 8.0


def prolong_rows(whole, share):
    coarse_rows = (row_index() * share + jnp.arange(share)) // 2
    return spread_yz(jnp.take(whole, coarse_rows, axis=0))


def whole_faces(volume):
    return face_list(jnp.pad(volume, 1))


def local(
    initial_saturation, permeability, porosity, source_rate, rock_type, water_endpoint, oil_endpoint
):
    slices = lax.axis_size("tm")
    slice_index = lax.axis_index("tm")
    water_block = lookup(rock_type, water_endpoint)
    oil_block = lookup(rock_type, oil_endpoint)
    restricted = restrict_blocks(jnp.stack([initial_saturation, permeability, porosity, source_rate]))
    whole = gather_grid(jnp.concatenate([restricted, jnp.stack([water_block, oil_block])]))
    start_coarse, permeability_upscaled, poro_coarse, source_coarse, water_coarse, oil_coarse = (
        whole[k] for k in range(6)
    )
    water_mobility, oil_mobility = mobilities(start_coarse, water_coarse, oil_coarse)
    transport_field_upscaled = permeability_upscaled * (water_mobility + oil_mobility)
    transmissibility_upscaled = [
        (transport_field_upscaled + exceeding_part) / 8.0
        for exceeding_part in whole_faces(transport_field_upscaled)
    ]
    diag_coarse = compress + accumulate_terms(transmissibility_upscaled)
    pressure_coarse = damping * source_coarse / diag_coarse
    for sweep_no in range(SWEEPS - 1):
        coupled = accumulate_terms(
            [
                conduct_face * exceeding_part
                for conduct_face, exceeding_part in zip(
                    transmissibility_upscaled, whole_faces(pressure_coarse)
                )
            ]
        )
        pressure_coarse = (
            pressure_coarse
            + damping * (source_coarse - (diag_coarse * pressure_coarse - coupled)) / diag_coarse
        )
    flows_coarse = [
        conduct_face * (pressure_coarse - exceeding_part)
        for conduct_face, exceeding_part in zip(transmissibility_upscaled, whole_faces(pressure_coarse))
    ]
    outgoing_coarse = accumulate_terms([jnp.maximum(outward, 0.0) for outward in flows_coarse])
    coarse_dt = FSTEPS * step_dt

    def coarse_step(coarse_state):
        frac, frac_slope = fractional(coarse_state, water_coarse, oil_coarse)
        flux_sum = upwind(frac, whole_faces(frac), flows_coarse)
        balance = (
            flux_sum - jnp.maximum(source_coarse, 0.0) - jnp.minimum(source_coarse, 0.0) * frac
        )
        slope_sum = poro_coarse / coarse_dt + jnp.abs(frac_slope) * (
            outgoing_coarse + jnp.maximum(-source_coarse, 0.0)
        )
        return coarse_state - balance / slope_sum

    def chain(corrections):

        def relay_round(turn_no, arrived):
            coarse_state = jnp.where(slice_index == 0, start_coarse, arrived)
            return passed_along(coarse_step(coarse_state) + corrections, "tm", 1)

        arrived = lax.fori_loop(0, slices - 1, relay_round, start_coarse)
        coarse_state = jnp.where(slice_index == 0, start_coarse, arrived)
        return (coarse_state, coarse_step(coarse_state))

    coarse_state = lax.fori_loop(
        0, slice_index, lambda turn_no, state: coarse_step(state), start_coarse
    )
    coarse_image = coarse_step(coarse_state)
    water_fine, oil_fine = prolong_blocks(jnp.stack([water_block, oil_block]))
    initial_rows, permeability, porosity, source_rate, water_fine, oil_fine = to_rows(
        jnp.stack([initial_saturation, permeability, porosity, source_rate, water_fine, oil_fine])
    )
    share = initial_rows.shape[0]
    starts = jnp.where(slice_index == 0, initial_rows, prolong_rows(coarse_state, share))
    previous_image = coarse_image
    ends = starts
    pressure = starts
    for parareal_no in range(PARAREAL):
        saturation = starts
        saturation, fine_pressure = fine_step(
            saturation, permeability, porosity, source_rate, water_fine, oil_fine
        )
        pressure = fine_pressure
        corrections = restrict_rows(saturation) - previous_image
        coarse_state, coarse_image = chain(corrections)
        ends = prolong_rows(coarse_image, share) + saturation - prolong_rows(previous_image, share)
        if parareal_no + 1 < PARAREAL:
            arrived_start = passed_along(ends, "tm", 1)
            starts = jnp.where(slice_index == 0, initial_rows, arrived_start)
        previous_image = coarse_image
    ends, pressure = from_rows(jnp.stack([ends, pressure]))
    return (ends[None], pressure[None])


def solution(mesh):
    in_specs = (
        P("sx", "sy", None),
        P("sx", "sy", None),
        P("sx", "sy", None),
        P("sx", "sy", None),
        P("sx", "sy", None),
        P(),
        P(),
    )
    out_specs = (P("tm", "sx", "sy", None), P("tm", "sx", "sy", None))
    return jax.shard_map(local, mesh=mesh, in_specs=in_specs, out_specs=out_specs, check_vma=False)
```

```python
import jax
import jax.numpy as jnp
from jax import lax
from jax.sharding import PartitionSpec as P

FSTEPS = 1
NEWTON = 2
CG_ITERS = 3
SWEEPS = 3
PARAREAL = 2
ROCKS = 4


mu_water = 1.0
mu_oil = 4.0
compress = 0.05
step_dt = 0.25
damping = 0.8


def extended(array, sides, width):
    for axis, dim in sides:
        size, length = (lax.axis_size(axis), array.shape[dim])
        up = [(i, (i + 1) % size) for i in range(size - 1)]
        down = [(j, i) for i, j in up]
        last = lax.slice_in_dim(array, length - width, length, axis=dim)
        initial = lax.slice_in_dim(array, 0, width, axis=dim)
        before = lax.ppermute(last, axis, up)
        after = lax.ppermute(initial, axis, down)
        array = jnp.concatenate([before, array, after], axis=dim)
    return array


def passed_along(value, axis, steps):
    count = lax.axis_size(axis)
    initial, last = (max(0, -steps), min(count, count - steps))
    return lax.ppermute(value, axis, [(source, source + steps) for source in range(initial, last)])


def lookup(rock_cells, end_values):
    summed_total = jnp.zeros(rock_cells.shape, end_values.dtype)
    for rock_kind in range(ROCKS):
        summed_total = summed_total + jnp.where(
            rock_cells == rock_kind, end_values[rock_kind], jnp.zeros((), end_values.dtype)
        )
    return summed_total


def restrict(volume):
    return volume.reshape(
        volume.shape[0] // 2, 2, volume.shape[1] // 2, 2, volume.shape[2] // 2, 2
    ).mean(axis=(1, 3, 5))


def prolong(volume):
    first, second, third = volume.shape
    spread_out = jnp.broadcast_to(
        volume[:, None, :, None, :, None], (first, 2, second, 2, third, 2)
    )
    return spread_out.reshape(2 * first, 2 * second, 2 * third)


def pair_matrix(count):
    rows = lax.broadcasted_iota(jnp.int32, (count, 2 * count), 0)
    cols = lax.broadcasted_iota(jnp.int32, (count, 2 * count), 1)
    return (cols // 2 == rows).astype(jnp.float32)


def sum_pairs_yz(volume):
    length_y, depth_z = volume.shape[-2:]
    lead = volume.shape[:-2]
    flat = volume.reshape((-1, length_y, depth_z))
    half_z = jnp.einsum("bkz,wz->bkw", flat, pair_matrix(depth_z // 2), precision=lax.Precision.HIGHEST)
    half_y = jnp.einsum("yk,bkw->byw", pair_matrix(length_y // 2), half_z, precision=lax.Precision.HIGHEST)
    return half_y.reshape(lead + (length_y // 2, depth_z // 2))


def spread_yz(volume):
    length_y, depth_z = volume.shape[-2:]
    lead = volume.shape[:-2]
    flat = volume.reshape((-1, length_y, depth_z))
    wide_z = jnp.einsum("bkz,zw->bkw", flat, pair_matrix(depth_z), precision=lax.Precision.HIGHEST)
    wide_y = jnp.einsum("ky,bkw->byw", pair_matrix(length_y), wide_z, precision=lax.Precision.HIGHEST)
    return wide_y.reshape(lead + (2 * length_y, 2 * depth_z))


def restrict_blocks(volume):
    fields, length_x, length_y, depth_z = volume.shape
    paired_x = volume.reshape(fields, length_x // 2, 2, length_y, depth_z).sum(axis=2)
    return sum_pairs_yz(paired_x) / 8.0


def prolong_blocks(volume):
    fields, length_x, length_y, depth_z = volume.shape
    spread = spread_yz(volume)
    spread = jnp.broadcast_to(spread[:, :, None], (fields, length_x, 2) + spread.shape[2:])
    return spread.reshape((fields, 2 * length_x) + spread.shape[3:])


def pad_depth(volume):
    return jnp.pad(volume, ((0, 0), (0, 0), (1, 1)))


def face_list(padded):
    return [
        padded[2:, 1:-1, 1:-1],
        padded[:-2, 1:-1, 1:-1],
        padded[1:-1, 2:, 1:-1],
        padded[1:-1, :-2, 1:-1],
        padded[1:-1, 1:-1, 2:],
        padded[1:-1, 1:-1, :-2],
    ]


ROW_AXES = ("sx", "sy")


def row_halo(volume):
    count = lax.axis_size("sx") * lax.axis_size("sy")
    up = [(i, i + 1) for i in range(count - 1)]
    down = [(i + 1, i) for i in range(count - 1)]
    before = lax.ppermute(volume[-1:], ROW_AXES, up)
    after = lax.ppermute(volume[:1], ROW_AXES, down)
    return jnp.concatenate([before, volume, after], axis=0)


def row_faces(volume):
    return face_list(jnp.pad(row_halo(volume), ((0, 0), (1, 1), (1, 1))))


def face_mobility_values(volume):
    return row_faces(volume)


def direction_spread(volume):
    return extended(volume, (("sx", 0), ("sy", 1)), 1)


def pressure_faces(volume):
    return row_faces(volume)


def flow_faces(volume):
    return row_faces(volume)


def build_face_tables(volume):
    return face_list(pad_depth(extended(volume, (("sx", 0), ("sy", 1)), 1)))


def coarse_faces(volume):
    return face_list(pad_depth(extended(volume, (("sx", 0), ("sy", 1)), 1)))


def accumulate_terms(summand_terms):
    summed_total = summand_terms[0]
    for summand_term in summand_terms[1:]:
        summed_total = summed_total + summand_term
    return summed_total


def mobilities(saturation, water_end, oil_end):
    water_mobility = water_end * saturation * saturation / mu_water
    oil_mobility = oil_end * (1.0 - saturation) * (1.0 - saturation) / mu_oil
    return (water_mobility, oil_mobility)


def fractional(saturation, water_end, oil_end):
    water_mobility, oil_mobility = mobilities(saturation, water_end, oil_end)
    mobility = water_mobility + oil_mobility
    water_slope = 2.0 * water_end * saturation / mu_water
    oil_slope = -2.0 * oil_end * (1.0 - saturation) / mu_oil
    return (
        water_mobility / mobility,
        (water_slope * oil_mobility - water_mobility * oil_slope) / (mobility * mobility),
    )


def upwind(frac, frac_beyond, outflows):
    return accumulate_terms(
        [
            jnp.maximum(outward, 0.0) * frac + jnp.minimum(outward, 0.0) * exceeding_part
            for outward, exceeding_part in zip(outflows, frac_beyond)
        ]
    )


def global_sums(values):
    count = lax.axis_size("sx") * lax.axis_size("sy")
    packed = jnp.broadcast_to(jnp.stack(values)[None], (count, len(values)))
    gathered = lax.all_to_all(packed, ("sx", "sy"), 0, 0, tiled=True)
    totals = jnp.sum(gathered, axis=0)
    return [totals[k] for k in range(len(values))]


def extended_faces(extended):
    return face_list(jnp.pad(extended, ((0, 0), (1, 1), (1, 1))))


def apply_operator(diagonal, transmissibility, vector):
    vector_rows = row_halo(vector)
    image = diagonal * vector - accumulate_terms(
        [
            conduct_face * exceeding_part
            for conduct_face, exceeding_part in zip(transmissibility, extended_faces(vector_rows))
        ]
    )
    return image, vector_rows


def solve_pressure(source_rate, diagonal, transmissibility):
    residual = source_rate
    solution = None
    for sweep_no in range(CG_ITERS):
        precond = residual / diagonal
        image, precond_rows = apply_operator(diagonal, transmissibility, precond)
        rho_next, curvature = global_sums([jnp.sum(residual * precond), jnp.sum(precond * image)])
        if sweep_no == 0:
            step_len = rho_next / curvature
            direction = precond_rows
            applied = image
            solution = step_len * direction
        else:
            ratio = rho_next / rho_now
            step_len = rho_next / (curvature - ratio * rho_next / step_len)
            direction = precond_rows + ratio * direction
            applied = image + ratio * applied
            solution = solution + step_len * direction
        if sweep_no + 1 < CG_ITERS:
            residual = residual - step_len * applied
        rho_now = rho_next
    return solution


def fine_step(sat_old, permeability, porosity, source_rate, water_end, oil_end, beside_fields):
    permeability_rows, water_rows, oil_rows, present_rows = beside_fields
    sat_rows = row_halo(sat_old)
    water_mobility, oil_mobility = mobilities(sat_rows, water_rows, oil_rows)
    transport_rows = permeability_rows * (water_mobility + oil_mobility)
    transport_field = transport_rows[1:-1]
    transmissibility = [
        0.5 * (transport_field + exceeding_part)
        for exceeding_part in extended_faces(transport_rows)
    ]
    diagonal = compress + accumulate_terms(transmissibility)
    pressure_rows = solve_pressure(source_rate, diagonal, transmissibility)
    pressure = pressure_rows[1:-1]
    beside = extended_faces(pressure_rows)
    outflows = [
        conduct_face * (pressure - exceeding_part)
        for conduct_face, exceeding_part in zip(transmissibility, beside)
    ]
    outgoing = accumulate_terms([jnp.maximum(outward, 0.0) for outward in outflows])
    saturation = sat_old
    for newton_no in range(NEWTON):
        frac, frac_slope = fractional(saturation, water_end, oil_end)
        if newton_no == 0:
            frac_rows = jnp.where(present_rows, fractional(sat_rows, water_rows, oil_rows)[0], 0.0)
            frac_beyond = extended_faces(frac_rows)
        else:
            frac_beyond = flow_faces(frac)
        flux_sum = upwind(frac, frac_beyond, outflows)
        balance = (
            porosity * (saturation - sat_old) / step_dt
            + flux_sum
            - jnp.maximum(source_rate, 0.0)
            - jnp.minimum(source_rate, 0.0) * frac
        )
        slope_sum = porosity / step_dt + jnp.abs(frac_slope) * (
            outgoing + jnp.maximum(-source_rate, 0.0)
        )
        saturation = saturation - balance / slope_sum
    return (saturation, pressure)


def gather_grid(blocks):
    rows, cols = (lax.axis_size("sx"), lax.axis_size("sy"))
    packed = jnp.broadcast_to(blocks[None], (rows * cols,) + blocks.shape)
    gathered = lax.all_to_all(packed, ("sx", "sy"), 0, 0, tiled=True)
    fields, depth_x, depth_y, depth_z = blocks.shape
    gathered = gathered.reshape(rows, cols, fields, depth_x, depth_y, depth_z)
    gathered = gathered.transpose(2, 0, 3, 1, 4, 5)
    return gathered.reshape(fields, rows * depth_x, cols * depth_y, depth_z)


def own_block(whole, shape):
    corner = (lax.axis_index("sx") * shape[0], lax.axis_index("sy") * shape[1], 0)
    return lax.dynamic_slice(whole, corner, shape)


def to_rows(blocks):
    columns = lax.axis_size("sy")
    fields, depth_x, depth_y, depth_z = blocks.shape
    share = depth_x // columns
    packed = blocks.reshape(fields, columns, share, depth_y, depth_z).transpose(1, 0, 2, 3, 4)
    got = lax.all_to_all(packed, "sy", 0, 0, tiled=True)
    return got.transpose(1, 2, 0, 3, 4).reshape(fields, share, columns * depth_y, depth_z)


def from_rows(rows):
    columns = lax.axis_size("sy")
    fields, share, length_y, depth_z = rows.shape
    depth_y = length_y // columns
    packed = rows.reshape(fields, share, columns, depth_y, depth_z).transpose(2, 0, 1, 3, 4)
    got = lax.all_to_all(packed, "sy", 0, 0, tiled=True)
    return got.transpose(1, 0, 2, 3, 4).reshape(fields, columns * share, depth_y, depth_z)


def row_index():
    return lax.axis_index("sx") * lax.axis_size("sy") + lax.axis_index("sy")


def restrict_rows(rows):
    share, length_y, depth_z = rows.shape
    partial = sum_pairs_yz(rows)
    count = lax.axis_size("sx") * lax.axis_size("sy")
    packed = jnp.broadcast_to(partial[None], (count,) + partial.shape)
    gathered = lax.all_to_all(packed, ROW_AXES, 0, 0, tiled=True)
    gathered = gathered.reshape(count * share // 2, 2, length_y // 2, depth_z // 2)
    return gathered.sum(axis=1) / 8.0


def prolong_rows(whole, share):
    coarse_rows = (row_index() * share + jnp.arange(share)) // 2
    return spread_yz(jnp.take(whole, coarse_rows, axis=0))


def whole_faces(volume):
    return face_list(jnp.pad(volume, 1))


def local(
    initial_saturation, permeability, porosity, source_rate, rock_type, water_endpoint, oil_endpoint
):
    slices = lax.axis_size("tm")
    slice_index = lax.axis_index("tm")
    water_block = lookup(rock_type, water_endpoint)
    oil_block = lookup(rock_type, oil_endpoint)
    restricted = restrict_blocks(jnp.stack([initial_saturation, permeability, porosity, source_rate]))
    whole = gather_grid(jnp.concatenate([restricted, jnp.stack([water_block, oil_block])]))
    start_coarse, permeability_upscaled, poro_coarse, source_coarse, water_coarse, oil_coarse = (
        whole[k] for k in range(6)
    )
    water_mobility, oil_mobility = mobilities(start_coarse, water_coarse, oil_coarse)
    transport_field_upscaled = permeability_upscaled * (water_mobility + oil_mobility)
    transmissibility_upscaled = [
        (transport_field_upscaled + exceeding_part) / 8.0
        for exceeding_part in whole_faces(transport_field_upscaled)
    ]
    diag_coarse = compress + accumulate_terms(transmissibility_upscaled)
    pressure_coarse = damping * source_coarse / diag_coarse
    for sweep_no in range(SWEEPS - 1):
        coupled = accumulate_terms(
            [
                conduct_face * exceeding_part
                for conduct_face, exceeding_part in zip(
                    transmissibility_upscaled, whole_faces(pressure_coarse)
                )
            ]
        )
        pressure_coarse = (
            pressure_coarse
            + damping * (source_coarse - (diag_coarse * pressure_coarse - coupled)) / diag_coarse
        )
    flows_coarse = [
        conduct_face * (pressure_coarse - exceeding_part)
        for conduct_face, exceeding_part in zip(transmissibility_upscaled, whole_faces(pressure_coarse))
    ]
    outgoing_coarse = accumulate_terms([jnp.maximum(outward, 0.0) for outward in flows_coarse])
    coarse_dt = FSTEPS * step_dt

    def coarse_step(coarse_state):
        frac, frac_slope = fractional(coarse_state, water_coarse, oil_coarse)
        flux_sum = upwind(frac, whole_faces(frac), flows_coarse)
        balance = (
            flux_sum - jnp.maximum(source_coarse, 0.0) - jnp.minimum(source_coarse, 0.0) * frac
        )
        slope_sum = poro_coarse / coarse_dt + jnp.abs(frac_slope) * (
            outgoing_coarse + jnp.maximum(-source_coarse, 0.0)
        )
        return coarse_state - balance / slope_sum

    def chain(corrections):

        def relay_round(turn_no, arrived):
            coarse_state = jnp.where(slice_index == 0, start_coarse, arrived)
            return passed_along(coarse_step(coarse_state) + corrections, "tm", 1)

        arrived = lax.fori_loop(0, slices - 1, relay_round, start_coarse)
        coarse_state = jnp.where(slice_index == 0, start_coarse, arrived)
        return (coarse_state, coarse_step(coarse_state))

    coarse_state = lax.fori_loop(
        0, slice_index, lambda turn_no, state: coarse_step(state), start_coarse
    )
    coarse_image = coarse_step(coarse_state)
    water_fine, oil_fine = prolong_blocks(jnp.stack([water_block, oil_block]))
    initial_rows, permeability, porosity, source_rate, water_fine, oil_fine = to_rows(
        jnp.stack([initial_saturation, permeability, porosity, source_rate, water_fine, oil_fine])
    )
    share = initial_rows.shape[0]
    stacked_rows = row_halo(jnp.stack([permeability, water_fine, oil_fine]).transpose(1, 0, 2, 3))
    stacked_rows = stacked_rows.transpose(1, 0, 2, 3)
    count = lax.axis_size("sx") * lax.axis_size("sy")
    row_number = lax.broadcasted_iota(jnp.int32, (share + 2, 1, 1), 0) - 1 + row_index() * share
    present_rows = (row_number >= 0) & (row_number < count * share)
    beside_fields = (stacked_rows[0], stacked_rows[1], stacked_rows[2], present_rows)
    starts = jnp.where(slice_index == 0, initial_rows, prolong_rows(coarse_state, share))
    previous_image = coarse_image
    ends = starts
    pressure = starts
    for parareal_no in range(PARAREAL):
        saturation = starts
        saturation, fine_pressure = fine_step(
            saturation, permeability, porosity, source_rate, water_fine, oil_fine, beside_fields
        )
        pressure = fine_pressure
        corrections = restrict_rows(saturation) - previous_image
        coarse_state, coarse_image = chain(corrections)
        ends = prolong_rows(coarse_image, share) + saturation - prolong_rows(previous_image, share)
        if parareal_no + 1 < PARAREAL:
            arrived_start = passed_along(ends, "tm", 1)
            starts = jnp.where(slice_index == 0, initial_rows, arrived_start)
        previous_image = coarse_image
    ends, pressure = from_rows(jnp.stack([ends, pressure]))
    return (ends[None], pressure[None])


def solution(mesh):
    in_specs = (
        P("sx", "sy", None),
        P("sx", "sy", None),
        P("sx", "sy", None),
        P("sx", "sy", None),
        P("sx", "sy", None),
        P(),
        P(),
    )
    out_specs = (P("tm", "sx", "sy", None), P("tm", "sx", "sy", None))
    return jax.shard_map(local, mesh=mesh, in_specs=in_specs, out_specs=out_specs, check_vma=False)
```

```python
import jax
import jax.numpy as jnp
from jax import lax
from jax.sharding import PartitionSpec as P

FSTEPS = 1
NEWTON = 2
CG_ITERS = 3
SWEEPS = 3
PARAREAL = 2
ROCKS = 4


mu_water = 1.0
mu_oil = 4.0
compress = 0.05
step_dt = 0.25
damping = 0.8


def extended(array, sides, width):
    for axis, dim in sides:
        size, length = (lax.axis_size(axis), array.shape[dim])
        up = [(i, (i + 1) % size) for i in range(size - 1)]
        down = [(j, i) for i, j in up]
        last = lax.slice_in_dim(array, length - width, length, axis=dim)
        initial = lax.slice_in_dim(array, 0, width, axis=dim)
        before = lax.ppermute(last, axis, up)
        after = lax.ppermute(initial, axis, down)
        array = jnp.concatenate([before, array, after], axis=dim)
    return array


def passed_along(value, axis, steps):
    count = lax.axis_size(axis)
    initial, last = (max(0, -steps), min(count, count - steps))
    return lax.ppermute(value, axis, [(source, source + steps) for source in range(initial, last)])


def lookup(rock_cells, end_values):
    summed_total = jnp.zeros(rock_cells.shape, end_values.dtype)
    for rock_kind in range(ROCKS):
        summed_total = summed_total + jnp.where(
            rock_cells == rock_kind, end_values[rock_kind], jnp.zeros((), end_values.dtype)
        )
    return summed_total


def restrict(volume):
    return volume.reshape(
        volume.shape[0] // 2, 2, volume.shape[1] // 2, 2, volume.shape[2] // 2, 2
    ).mean(axis=(1, 3, 5))


def prolong(volume):
    first, second, third = volume.shape
    spread_out = jnp.broadcast_to(
        volume[:, None, :, None, :, None], (first, 2, second, 2, third, 2)
    )
    return spread_out.reshape(2 * first, 2 * second, 2 * third)


def pair_matrix(count):
    rows = lax.broadcasted_iota(jnp.int32, (count, 2 * count), 0)
    cols = lax.broadcasted_iota(jnp.int32, (count, 2 * count), 1)
    return (cols // 2 == rows).astype(jnp.float32)


def sum_pairs_yz(volume):
    length_y, depth_z = volume.shape[-2:]
    lead = volume.shape[:-2]
    flat = volume.reshape((-1, length_y, depth_z))
    half_z = jnp.einsum("bkz,wz->bkw", flat, pair_matrix(depth_z // 2), precision=lax.Precision.HIGHEST)
    half_y = jnp.einsum("yk,bkw->byw", pair_matrix(length_y // 2), half_z, precision=lax.Precision.HIGHEST)
    return half_y.reshape(lead + (length_y // 2, depth_z // 2))


def spread_yz(volume):
    length_y, depth_z = volume.shape[-2:]
    lead = volume.shape[:-2]
    flat = volume.reshape((-1, length_y, depth_z))
    wide_z = jnp.einsum("bkz,zw->bkw", flat, pair_matrix(depth_z), precision=lax.Precision.HIGHEST)
    wide_y = jnp.einsum("ky,bkw->byw", pair_matrix(length_y), wide_z, precision=lax.Precision.HIGHEST)
    return wide_y.reshape(lead + (2 * length_y, 2 * depth_z))


def restrict_blocks(volume):
    fields, length_x, length_y, depth_z = volume.shape
    paired_x = volume.reshape(fields, length_x // 2, 2, length_y, depth_z).sum(axis=2)
    return sum_pairs_yz(paired_x) / 8.0


def prolong_blocks(volume):
    fields, length_x, length_y, depth_z = volume.shape
    spread = spread_yz(volume)
    spread = jnp.broadcast_to(spread[:, :, None], (fields, length_x, 2) + spread.shape[2:])
    return spread.reshape((fields, 2 * length_x) + spread.shape[3:])


def pad_depth(volume):
    return jnp.pad(volume, ((0, 0), (0, 0), (1, 1)))


def face_list(padded):
    return [
        padded[2:, 1:-1, 1:-1],
        padded[:-2, 1:-1, 1:-1],
        padded[1:-1, 2:, 1:-1],
        padded[1:-1, :-2, 1:-1],
        padded[1:-1, 1:-1, 2:],
        padded[1:-1, 1:-1, :-2],
    ]


ROW_AXES = ("sx", "sy")


def row_halo(volume):
    count = lax.axis_size("sx") * lax.axis_size("sy")
    up = [(i, i + 1) for i in range(count - 1)]
    down = [(i + 1, i) for i in range(count - 1)]
    before = lax.ppermute(volume[-1:], ROW_AXES, up)
    after = lax.ppermute(volume[:1], ROW_AXES, down)
    return jnp.concatenate([before, volume, after], axis=0)


def row_faces(volume):
    return face_list(jnp.pad(row_halo(volume), ((0, 0), (1, 1), (1, 1))))


def face_mobility_values(volume):
    return row_faces(volume)


def direction_spread(volume):
    return extended(volume, (("sx", 0), ("sy", 1)), 1)


def pressure_faces(volume):
    return row_faces(volume)


def flow_faces(volume):
    return row_faces(volume)


def build_face_tables(volume):
    return face_list(pad_depth(extended(volume, (("sx", 0), ("sy", 1)), 1)))


def coarse_faces(volume):
    return face_list(pad_depth(extended(volume, (("sx", 0), ("sy", 1)), 1)))


def accumulate_terms(summand_terms):
    summed_total = summand_terms[0]
    for summand_term in summand_terms[1:]:
        summed_total = summed_total + summand_term
    return summed_total


def mobilities(saturation, water_end, oil_end):
    water_mobility = water_end * saturation * saturation / mu_water
    oil_mobility = oil_end * (1.0 - saturation) * (1.0 - saturation) / mu_oil
    return (water_mobility, oil_mobility)


def fractional(saturation, water_end, oil_end):
    water_mobility, oil_mobility = mobilities(saturation, water_end, oil_end)
    mobility = water_mobility + oil_mobility
    water_slope = 2.0 * water_end * saturation / mu_water
    oil_slope = -2.0 * oil_end * (1.0 - saturation) / mu_oil
    return (
        water_mobility / mobility,
        (water_slope * oil_mobility - water_mobility * oil_slope) / (mobility * mobility),
    )


def upwind(frac, frac_beyond, outflows):
    return accumulate_terms(
        [
            jnp.maximum(outward, 0.0) * frac + jnp.minimum(outward, 0.0) * exceeding_part
            for outward, exceeding_part in zip(outflows, frac_beyond)
        ]
    )


def global_sums(values):
    count = lax.axis_size("sx") * lax.axis_size("sy")
    packed = jnp.broadcast_to(jnp.stack(values)[None], (count, len(values)))
    gathered = lax.all_to_all(packed, ("sx", "sy"), 0, 0, tiled=True)
    totals = jnp.sum(gathered, axis=0)
    return [totals[k] for k in range(len(values))]


def extended_faces(extended):
    return face_list(jnp.pad(extended, ((0, 0), (1, 1), (1, 1))))


def apply_operator(diagonal, transmissibility, vector):
    vector_rows = row_halo(vector)
    image = diagonal * vector - accumulate_terms(
        [
            conduct_face * exceeding_part
            for conduct_face, exceeding_part in zip(transmissibility, extended_faces(vector_rows))
        ]
    )
    return image, vector_rows


def solve_pressure(source_rate, diagonal, transmissibility):
    residual = source_rate
    solution = None
    for sweep_no in range(CG_ITERS):
        precond = residual / diagonal
        image, precond_rows = apply_operator(diagonal, transmissibility, precond)
        rho_next, curvature = global_sums([jnp.sum(residual * precond), jnp.sum(precond * image)])
        if sweep_no == 0:
            step_len = rho_next / curvature
            direction = precond_rows
            applied = image
            solution = step_len * direction
        else:
            ratio = rho_next / rho_now
            step_len = rho_next / (curvature - ratio * rho_next / step_len)
            direction = precond_rows + ratio * direction
            applied = image + ratio * applied
            solution = solution + step_len * direction
        if sweep_no + 1 < CG_ITERS:
            residual = residual - step_len * applied
        rho_now = rho_next
    return solution


def fine_step(sat_old, permeability, porosity, source_rate, water_end, oil_end, beside_fields):
    permeability_rows, water_rows, oil_rows, present_rows = beside_fields
    sat_rows = row_halo(sat_old)
    water_mobility, oil_mobility = mobilities(sat_rows, water_rows, oil_rows)
    transport_rows = permeability_rows * (water_mobility + oil_mobility)
    transport_field = transport_rows[1:-1]
    transmissibility = [
        0.5 * (transport_field + exceeding_part)
        for exceeding_part in extended_faces(transport_rows)
    ]
    diagonal = compress + accumulate_terms(transmissibility)
    pressure_rows = solve_pressure(source_rate, diagonal, transmissibility)
    pressure = pressure_rows[1:-1]
    beside = extended_faces(pressure_rows)
    outflows = [
        conduct_face * (pressure - exceeding_part)
        for conduct_face, exceeding_part in zip(transmissibility, beside)
    ]
    outgoing = accumulate_terms([jnp.maximum(outward, 0.0) for outward in outflows])
    saturation = sat_old
    for newton_no in range(NEWTON):
        frac, frac_slope = fractional(saturation, water_end, oil_end)
        if newton_no == 0:
            frac_rows = jnp.where(present_rows, fractional(sat_rows, water_rows, oil_rows)[0], 0.0)
            frac_beyond = extended_faces(frac_rows)
        else:
            frac_beyond = flow_faces(frac)
        flux_sum = upwind(frac, frac_beyond, outflows)
        balance = (
            porosity * (saturation - sat_old) / step_dt
            + flux_sum
            - jnp.maximum(source_rate, 0.0)
            - jnp.minimum(source_rate, 0.0) * frac
        )
        slope_sum = porosity / step_dt + jnp.abs(frac_slope) * (
            outgoing + jnp.maximum(-source_rate, 0.0)
        )
        saturation = saturation - balance / slope_sum
    return (saturation, pressure)


def gather_grid(blocks):
    rows, cols = (lax.axis_size("sx"), lax.axis_size("sy"))
    packed = jnp.broadcast_to(blocks[None], (rows * cols,) + blocks.shape)
    gathered = lax.all_to_all(packed, ("sx", "sy"), 0, 0, tiled=True)
    fields, depth_x, depth_y, depth_z = blocks.shape
    gathered = gathered.reshape(rows, cols, fields, depth_x, depth_y, depth_z)
    gathered = gathered.transpose(2, 0, 3, 1, 4, 5)
    return gathered.reshape(fields, rows * depth_x, cols * depth_y, depth_z)


def own_block(whole, shape):
    corner = (lax.axis_index("sx") * shape[0], lax.axis_index("sy") * shape[1], 0)
    return lax.dynamic_slice(whole, corner, shape)


def to_rows(blocks):
    columns = lax.axis_size("sy")
    fields, depth_x, depth_y, depth_z = blocks.shape
    share = depth_x // columns
    packed = blocks.reshape(fields, columns, share, depth_y, depth_z).transpose(1, 0, 2, 3, 4)
    got = lax.all_to_all(packed, "sy", 0, 0, tiled=True)
    return got.transpose(1, 2, 0, 3, 4).reshape(fields, share, columns * depth_y, depth_z)


def from_rows(rows):
    columns = lax.axis_size("sy")
    fields, share, length_y, depth_z = rows.shape
    depth_y = length_y // columns
    packed = rows.reshape(fields, share, columns, depth_y, depth_z).transpose(2, 0, 1, 3, 4)
    got = lax.all_to_all(packed, "sy", 0, 0, tiled=True)
    return got.transpose(1, 0, 2, 3, 4).reshape(fields, columns * share, depth_y, depth_z)


def row_index():
    return lax.axis_index("sx") * lax.axis_size("sy") + lax.axis_index("sy")


def restrict_rows(rows):
    share, length_y, depth_z = rows.shape
    partial = sum_pairs_yz(rows)
    count = lax.axis_size("sx") * lax.axis_size("sy")
    packed = jnp.broadcast_to(partial[None], (count,) + partial.shape)
    gathered = lax.all_to_all(packed, ROW_AXES, 0, 0, tiled=True)
    gathered = gathered.reshape(count * share // 2, 2, length_y // 2, depth_z // 2)
    return gathered.sum(axis=1) / 8.0


def prolong_rows(whole, share):
    coarse_rows = (row_index() * share + jnp.arange(share)) // 2
    return spread_yz(jnp.take(whole, coarse_rows, axis=0))


def whole_faces(volume):
    return face_list(jnp.pad(volume, 1))


def local(
    initial_saturation, permeability, porosity, source_rate, rock_type, water_endpoint, oil_endpoint
):
    slices = lax.axis_size("tm")
    slice_index = lax.axis_index("tm")
    water_block = lookup(rock_type, water_endpoint)
    oil_block = lookup(rock_type, oil_endpoint)
    restricted = restrict_blocks(jnp.stack([initial_saturation, permeability, porosity, source_rate]))
    whole = gather_grid(jnp.concatenate([restricted, jnp.stack([water_block, oil_block])]))
    start_coarse, permeability_upscaled, poro_coarse, source_coarse, water_coarse, oil_coarse = (
        whole[k] for k in range(6)
    )
    water_mobility, oil_mobility = mobilities(start_coarse, water_coarse, oil_coarse)
    transport_field_upscaled = permeability_upscaled * (water_mobility + oil_mobility)
    transmissibility_upscaled = [
        (transport_field_upscaled + exceeding_part) / 8.0
        for exceeding_part in whole_faces(transport_field_upscaled)
    ]
    diag_coarse = compress + accumulate_terms(transmissibility_upscaled)
    pressure_coarse = damping * source_coarse / diag_coarse
    for sweep_no in range(SWEEPS - 1):
        coupled = accumulate_terms(
            [
                conduct_face * exceeding_part
                for conduct_face, exceeding_part in zip(
                    transmissibility_upscaled, whole_faces(pressure_coarse)
                )
            ]
        )
        pressure_coarse = (
            pressure_coarse
            + damping * (source_coarse - (diag_coarse * pressure_coarse - coupled)) / diag_coarse
        )
    flows_coarse = [
        conduct_face * (pressure_coarse - exceeding_part)
        for conduct_face, exceeding_part in zip(transmissibility_upscaled, whole_faces(pressure_coarse))
    ]
    outgoing_coarse = accumulate_terms([jnp.maximum(outward, 0.0) for outward in flows_coarse])
    coarse_dt = FSTEPS * step_dt

    def coarse_step(coarse_state):
        frac, frac_slope = fractional(coarse_state, water_coarse, oil_coarse)
        flux_sum = upwind(frac, whole_faces(frac), flows_coarse)
        balance = (
            flux_sum - jnp.maximum(source_coarse, 0.0) - jnp.minimum(source_coarse, 0.0) * frac
        )
        slope_sum = poro_coarse / coarse_dt + jnp.abs(frac_slope) * (
            outgoing_coarse + jnp.maximum(-source_coarse, 0.0)
        )
        return coarse_state - balance / slope_sum

    def chain(corrections):
        packed = jnp.broadcast_to(corrections[None], (slices,) + corrections.shape)
        every = lax.all_to_all(packed, "tm", 0, 0, tiled=True)

        def corrected_step(turn_no, coarse_state):
            return coarse_step(coarse_state) + every[turn_no]

        coarse_state = lax.fori_loop(0, slice_index, corrected_step, start_coarse)
        return (coarse_state, coarse_step(coarse_state))

    coarse_state = lax.fori_loop(
        0, slice_index, lambda turn_no, state: coarse_step(state), start_coarse
    )
    coarse_image = coarse_step(coarse_state)
    water_fine, oil_fine = prolong_blocks(jnp.stack([water_block, oil_block]))
    initial_rows, permeability, porosity, source_rate, water_fine, oil_fine = to_rows(
        jnp.stack([initial_saturation, permeability, porosity, source_rate, water_fine, oil_fine])
    )
    share = initial_rows.shape[0]
    stacked_rows = row_halo(jnp.stack([permeability, water_fine, oil_fine]).transpose(1, 0, 2, 3))
    stacked_rows = stacked_rows.transpose(1, 0, 2, 3)
    count = lax.axis_size("sx") * lax.axis_size("sy")
    row_number = lax.broadcasted_iota(jnp.int32, (share + 2, 1, 1), 0) - 1 + row_index() * share
    present_rows = (row_number >= 0) & (row_number < count * share)
    beside_fields = (stacked_rows[0], stacked_rows[1], stacked_rows[2], present_rows)
    starts = jnp.where(slice_index == 0, initial_rows, prolong_rows(coarse_state, share))
    previous_image = coarse_image
    ends = starts
    pressure = starts
    for parareal_no in range(PARAREAL):
        saturation = starts
        saturation, fine_pressure = fine_step(
            saturation, permeability, porosity, source_rate, water_fine, oil_fine, beside_fields
        )
        pressure = fine_pressure
        corrections = restrict_rows(saturation) - previous_image
        coarse_state, coarse_image = chain(corrections)
        ends = prolong_rows(coarse_image, share) + saturation - prolong_rows(previous_image, share)
        if parareal_no + 1 < PARAREAL:
            arrived_start = passed_along(ends, "tm", 1)
            starts = jnp.where(slice_index == 0, initial_rows, arrived_start)
        previous_image = coarse_image
    ends, pressure = from_rows(jnp.stack([ends, pressure]))
    return (ends[None], pressure[None])


def solution(mesh):
    in_specs = (
        P("sx", "sy", None),
        P("sx", "sy", None),
        P("sx", "sy", None),
        P("sx", "sy", None),
        P("sx", "sy", None),
        P(),
        P(),
    )
    out_specs = (P("tm", "sx", "sy", None), P("tm", "sx", "sy", None))
    return jax.shard_map(local, mesh=mesh, in_specs=in_specs, out_specs=out_specs, check_vma=False)
```

```python
import jax
import jax.numpy as jnp
from jax import lax
from jax.sharding import PartitionSpec as P

FSTEPS = 1
NEWTON = 2
CG_ITERS = 3
SWEEPS = 3
PARAREAL = 2
ROCKS = 4


mu_water = 1.0
mu_oil = 4.0
compress = 0.05
step_dt = 0.25
damping = 0.8


def extended(array, sides, width):
    for axis, dim in sides:
        size, length = (lax.axis_size(axis), array.shape[dim])
        up = [(i, (i + 1) % size) for i in range(size - 1)]
        down = [(j, i) for i, j in up]
        last = lax.slice_in_dim(array, length - width, length, axis=dim)
        initial = lax.slice_in_dim(array, 0, width, axis=dim)
        before = lax.ppermute(last, axis, up)
        after = lax.ppermute(initial, axis, down)
        array = jnp.concatenate([before, array, after], axis=dim)
    return array


def passed_along(value, axis, steps):
    count = lax.axis_size(axis)
    initial, last = (max(0, -steps), min(count, count - steps))
    return lax.ppermute(value, axis, [(source, source + steps) for source in range(initial, last)])


def lookup(rock_cells, end_values):
    summed_total = jnp.zeros(rock_cells.shape, end_values.dtype)
    for rock_kind in range(ROCKS):
        summed_total = summed_total + jnp.where(
            rock_cells == rock_kind, end_values[rock_kind], jnp.zeros((), end_values.dtype)
        )
    return summed_total


def restrict(volume):
    return volume.reshape(
        volume.shape[0] // 2, 2, volume.shape[1] // 2, 2, volume.shape[2] // 2, 2
    ).mean(axis=(1, 3, 5))


def prolong(volume):
    first, second, third = volume.shape
    spread_out = jnp.broadcast_to(
        volume[:, None, :, None, :, None], (first, 2, second, 2, third, 2)
    )
    return spread_out.reshape(2 * first, 2 * second, 2 * third)


def pair_matrix(count):
    rows = lax.broadcasted_iota(jnp.int32, (count, 2 * count), 0)
    cols = lax.broadcasted_iota(jnp.int32, (count, 2 * count), 1)
    return (cols // 2 == rows).astype(jnp.float32)


def sum_pairs_yz(volume):
    length_y, depth_z = volume.shape[-2:]
    lead = volume.shape[:-2]
    flat = volume.reshape((-1, length_y, depth_z))
    half_z = jnp.einsum("bkz,wz->bkw", flat, pair_matrix(depth_z // 2), precision=lax.Precision.HIGHEST)
    half_y = jnp.einsum("yk,bkw->byw", pair_matrix(length_y // 2), half_z, precision=lax.Precision.HIGHEST)
    return half_y.reshape(lead + (length_y // 2, depth_z // 2))


def spread_yz(volume):
    length_y, depth_z = volume.shape[-2:]
    lead = volume.shape[:-2]
    flat = volume.reshape((-1, length_y, depth_z))
    wide_z = jnp.einsum("bkz,zw->bkw", flat, pair_matrix(depth_z), precision=lax.Precision.HIGHEST)
    wide_y = jnp.einsum("ky,bkw->byw", pair_matrix(length_y), wide_z, precision=lax.Precision.HIGHEST)
    return wide_y.reshape(lead + (2 * length_y, 2 * depth_z))


def restrict_blocks(volume):
    fields, length_x, length_y, depth_z = volume.shape
    paired_x = volume.reshape(fields, length_x // 2, 2, length_y, depth_z).sum(axis=2)
    return sum_pairs_yz(paired_x) / 8.0


def prolong_blocks(volume):
    fields, length_x, length_y, depth_z = volume.shape
    spread = spread_yz(volume)
    spread = jnp.broadcast_to(spread[:, :, None], (fields, length_x, 2) + spread.shape[2:])
    return spread.reshape((fields, 2 * length_x) + spread.shape[3:])


def pad_depth(volume):
    return jnp.pad(volume, ((0, 0), (0, 0), (1, 1)))


def face_list(padded):
    return [
        padded[2:, 1:-1, 1:-1],
        padded[:-2, 1:-1, 1:-1],
        padded[1:-1, 2:, 1:-1],
        padded[1:-1, :-2, 1:-1],
        padded[1:-1, 1:-1, 2:],
        padded[1:-1, 1:-1, :-2],
    ]


ROW_AXES = ("sx", "sy")


def row_halo(volume):
    count = lax.axis_size("sx") * lax.axis_size("sy")
    up = [(i, i + 1) for i in range(count - 1)]
    down = [(i + 1, i) for i in range(count - 1)]
    before = lax.ppermute(volume[-1:], ROW_AXES, up)
    after = lax.ppermute(volume[:1], ROW_AXES, down)
    return jnp.concatenate([before, volume, after], axis=0)


def row_faces(volume):
    return face_list(jnp.pad(row_halo(volume), ((0, 0), (1, 1), (1, 1))))


def face_mobility_values(volume):
    return row_faces(volume)


def direction_spread(volume):
    return extended(volume, (("sx", 0), ("sy", 1)), 1)


def pressure_faces(volume):
    return row_faces(volume)


def flow_faces(volume):
    return row_faces(volume)


def build_face_tables(volume):
    return face_list(pad_depth(extended(volume, (("sx", 0), ("sy", 1)), 1)))


def coarse_faces(volume):
    return face_list(pad_depth(extended(volume, (("sx", 0), ("sy", 1)), 1)))


def accumulate_terms(summand_terms):
    summed_total = summand_terms[0]
    for summand_term in summand_terms[1:]:
        summed_total = summed_total + summand_term
    return summed_total


def mobilities(saturation, water_end, oil_end):
    water_mobility = water_end * saturation * saturation / mu_water
    oil_mobility = oil_end * (1.0 - saturation) * (1.0 - saturation) / mu_oil
    return (water_mobility, oil_mobility)


def fractional(saturation, water_end, oil_end):
    water_mobility, oil_mobility = mobilities(saturation, water_end, oil_end)
    mobility = water_mobility + oil_mobility
    water_slope = 2.0 * water_end * saturation / mu_water
    oil_slope = -2.0 * oil_end * (1.0 - saturation) / mu_oil
    return (
        water_mobility / mobility,
        (water_slope * oil_mobility - water_mobility * oil_slope) / (mobility * mobility),
    )


def upwind(frac, frac_beyond, outflows):
    return accumulate_terms(
        [
            jnp.maximum(outward, 0.0) * frac + jnp.minimum(outward, 0.0) * exceeding_part
            for outward, exceeding_part in zip(outflows, frac_beyond)
        ]
    )


def global_sums(values):
    count = lax.axis_size("sx") * lax.axis_size("sy")
    packed = jnp.broadcast_to(jnp.stack(values)[None], (count, len(values)))
    gathered = lax.all_to_all(packed, ("sx", "sy"), 0, 0, tiled=True)
    totals = jnp.sum(gathered, axis=0)
    return [totals[k] for k in range(len(values))]


def extended_faces(extended):
    return face_list(jnp.pad(extended, ((0, 0), (1, 1), (1, 1))))


def apply_operator(diagonal, transmissibility, vector):
    vector_rows = row_halo(vector)
    image = diagonal * vector - accumulate_terms(
        [
            conduct_face * exceeding_part
            for conduct_face, exceeding_part in zip(transmissibility, extended_faces(vector_rows))
        ]
    )
    return image, vector_rows


def solve_pressure(source_rate, diagonal, transmissibility):
    residual = source_rate
    solution = None
    for sweep_no in range(CG_ITERS):
        precond = residual / diagonal
        image, precond_rows = apply_operator(diagonal, transmissibility, precond)
        rho_next, curvature = global_sums([jnp.sum(residual * precond), jnp.sum(precond * image)])
        if sweep_no == 0:
            step_len = rho_next / curvature
            direction = precond_rows
            applied = image
            solution = step_len * direction
        else:
            ratio = rho_next / rho_now
            step_len = rho_next / (curvature - ratio * rho_next / step_len)
            direction = precond_rows + ratio * direction
            applied = image + ratio * applied
            solution = solution + step_len * direction
        if sweep_no + 1 < CG_ITERS:
            residual = residual - step_len * applied
        rho_now = rho_next
    return solution


def fine_step(sat_old, permeability, porosity, source_rate, water_end, oil_end, beside_fields):
    permeability_rows, water_rows, oil_rows, present_rows = beside_fields
    sat_rows = row_halo(sat_old)
    water_mobility, oil_mobility = mobilities(sat_rows, water_rows, oil_rows)
    transport_rows = permeability_rows * (water_mobility + oil_mobility)
    transport_field = transport_rows[1:-1]
    transmissibility = [
        0.5 * (transport_field + exceeding_part)
        for exceeding_part in extended_faces(transport_rows)
    ]
    diagonal = compress + accumulate_terms(transmissibility)
    pressure_rows = solve_pressure(source_rate, diagonal, transmissibility)
    pressure = pressure_rows[1:-1]
    beside = extended_faces(pressure_rows)
    outflows = [
        conduct_face * (pressure - exceeding_part)
        for conduct_face, exceeding_part in zip(transmissibility, beside)
    ]
    outgoing = accumulate_terms([jnp.maximum(outward, 0.0) for outward in outflows])
    saturation = sat_old
    for newton_no in range(NEWTON):
        frac, frac_slope = fractional(saturation, water_end, oil_end)
        if newton_no == 0:
            frac_rows = jnp.where(present_rows, fractional(sat_rows, water_rows, oil_rows)[0], 0.0)
            frac_beyond = extended_faces(frac_rows)
        else:
            frac_beyond = flow_faces(frac)
        flux_sum = upwind(frac, frac_beyond, outflows)
        balance = (
            porosity * (saturation - sat_old) / step_dt
            + flux_sum
            - jnp.maximum(source_rate, 0.0)
            - jnp.minimum(source_rate, 0.0) * frac
        )
        slope_sum = porosity / step_dt + jnp.abs(frac_slope) * (
            outgoing + jnp.maximum(-source_rate, 0.0)
        )
        saturation = saturation - balance / slope_sum
    return (saturation, pressure)


def gather_grid(blocks):
    rows, cols = (lax.axis_size("sx"), lax.axis_size("sy"))
    packed = jnp.broadcast_to(blocks[None], (rows * cols,) + blocks.shape)
    gathered = lax.all_to_all(packed, ("sx", "sy"), 0, 0, tiled=True)
    fields, depth_x, depth_y, depth_z = blocks.shape
    gathered = gathered.reshape(rows, cols, fields, depth_x, depth_y, depth_z)
    gathered = gathered.transpose(2, 0, 3, 1, 4, 5)
    return gathered.reshape(fields, rows * depth_x, cols * depth_y, depth_z)


def own_block(whole, shape):
    corner = (lax.axis_index("sx") * shape[0], lax.axis_index("sy") * shape[1], 0)
    return lax.dynamic_slice(whole, corner, shape)


def to_rows(blocks):
    columns = lax.axis_size("sy")
    fields, depth_x, depth_y, depth_z = blocks.shape
    share = depth_x // columns
    packed = blocks.reshape(fields, columns, share, depth_y, depth_z).transpose(1, 0, 2, 3, 4)
    got = lax.all_to_all(packed, "sy", 0, 0, tiled=True)
    return got.transpose(1, 2, 0, 3, 4).reshape(fields, share, columns * depth_y, depth_z)


def from_rows(rows):
    columns = lax.axis_size("sy")
    fields, share, length_y, depth_z = rows.shape
    depth_y = length_y // columns
    packed = rows.reshape(fields, share, columns, depth_y, depth_z).transpose(2, 0, 1, 3, 4)
    got = lax.all_to_all(packed, "sy", 0, 0, tiled=True)
    return got.transpose(1, 0, 2, 3, 4).reshape(fields, columns * share, depth_y, depth_z)


def row_index():
    return lax.axis_index("sx") * lax.axis_size("sy") + lax.axis_index("sy")


def restrict_rows(rows):
    share, length_y, depth_z = rows.shape
    partial = sum_pairs_yz(rows)
    count = lax.axis_size("sx") * lax.axis_size("sy")
    packed = jnp.broadcast_to(partial[None], (count,) + partial.shape)
    gathered = lax.all_to_all(packed, ROW_AXES, 0, 0, tiled=True)
    gathered = gathered.reshape(count * share // 2, 2, length_y // 2, depth_z // 2)
    return gathered.sum(axis=1) / 8.0


def prolong_rows(whole, share):
    coarse_rows = (row_index() * share + jnp.arange(share)) // 2
    return spread_yz(jnp.take(whole, coarse_rows, axis=0))


def whole_faces(volume):
    return face_list(jnp.pad(volume, 1))


def local(
    initial_saturation, permeability, porosity, source_rate, rock_type, water_endpoint, oil_endpoint
):
    slices = lax.axis_size("tm")
    slice_index = lax.axis_index("tm")
    water_block = lookup(rock_type, water_endpoint)
    oil_block = lookup(rock_type, oil_endpoint)
    restricted = restrict_blocks(jnp.stack([initial_saturation, permeability, porosity, source_rate]))
    whole = gather_grid(jnp.concatenate([restricted, jnp.stack([water_block, oil_block])]))
    start_coarse, permeability_upscaled, poro_coarse, source_coarse, water_coarse, oil_coarse = (
        whole[k] for k in range(6)
    )
    water_mobility, oil_mobility = mobilities(start_coarse, water_coarse, oil_coarse)
    transport_field_upscaled = permeability_upscaled * (water_mobility + oil_mobility)
    transmissibility_upscaled = [
        (transport_field_upscaled + exceeding_part) / 8.0
        for exceeding_part in whole_faces(transport_field_upscaled)
    ]
    diag_coarse = compress + accumulate_terms(transmissibility_upscaled)
    pressure_coarse = damping * source_coarse / diag_coarse
    for sweep_no in range(SWEEPS - 1):
        coupled = accumulate_terms(
            [
                conduct_face * exceeding_part
                for conduct_face, exceeding_part in zip(
                    transmissibility_upscaled, whole_faces(pressure_coarse)
                )
            ]
        )
        pressure_coarse = (
            pressure_coarse
            + damping * (source_coarse - (diag_coarse * pressure_coarse - coupled)) / diag_coarse
        )
    flows_coarse = [
        conduct_face * (pressure_coarse - exceeding_part)
        for conduct_face, exceeding_part in zip(transmissibility_upscaled, whole_faces(pressure_coarse))
    ]
    outgoing_coarse = accumulate_terms([jnp.maximum(outward, 0.0) for outward in flows_coarse])
    coarse_dt = FSTEPS * step_dt

    def coarse_step(coarse_state):
        frac, frac_slope = fractional(coarse_state, water_coarse, oil_coarse)
        flux_sum = upwind(frac, whole_faces(frac), flows_coarse)
        balance = (
            flux_sum - jnp.maximum(source_coarse, 0.0) - jnp.minimum(source_coarse, 0.0) * frac
        )
        slope_sum = poro_coarse / coarse_dt + jnp.abs(frac_slope) * (
            outgoing_coarse + jnp.maximum(-source_coarse, 0.0)
        )
        return coarse_state - balance / slope_sum

    def chain(corrections):
        ahead = corrections[None]
        collected = [jnp.zeros_like(ahead)]
        steps = 1
        while steps < slices:
            arrived = passed_along(ahead, "tm", steps)
            collected.insert(1, arrived)
            ahead = jnp.concatenate([arrived, ahead])
            steps *= 2
        ahead = jnp.concatenate(collected)
        offset = ahead.shape[0] - 1 - slice_index

        def corrected_step(turn_no, coarse_image):
            return coarse_step(coarse_image + ahead[turn_no + offset])

        coarse_image = lax.fori_loop(0, slice_index, corrected_step, start_coarse)
        coarse_state = coarse_image + ahead[slice_index + offset]
        return (coarse_state, coarse_step(coarse_state))

    coarse_state = lax.fori_loop(
        0, slice_index, lambda turn_no, state: coarse_step(state), start_coarse
    )
    coarse_image = coarse_step(coarse_state)
    water_fine, oil_fine = prolong_blocks(jnp.stack([water_block, oil_block]))
    initial_rows, permeability, porosity, source_rate, water_fine, oil_fine = to_rows(
        jnp.stack([initial_saturation, permeability, porosity, source_rate, water_fine, oil_fine])
    )
    share = initial_rows.shape[0]
    stacked_rows = row_halo(jnp.stack([permeability, water_fine, oil_fine]).transpose(1, 0, 2, 3))
    stacked_rows = stacked_rows.transpose(1, 0, 2, 3)
    count = lax.axis_size("sx") * lax.axis_size("sy")
    row_number = lax.broadcasted_iota(jnp.int32, (share + 2, 1, 1), 0) - 1 + row_index() * share
    present_rows = (row_number >= 0) & (row_number < count * share)
    beside_fields = (stacked_rows[0], stacked_rows[1], stacked_rows[2], present_rows)
    starts = jnp.where(slice_index == 0, initial_rows, prolong_rows(coarse_state, share))
    previous_image = coarse_image
    ends = starts
    pressure = starts
    for parareal_no in range(PARAREAL):
        saturation = starts
        saturation, fine_pressure = fine_step(
            saturation, permeability, porosity, source_rate, water_fine, oil_fine, beside_fields
        )
        pressure = fine_pressure
        corrections = restrict_rows(saturation) - previous_image
        coarse_state, coarse_image = chain(corrections)
        ends = prolong_rows(coarse_image, share) + saturation - prolong_rows(previous_image, share)
        if parareal_no + 1 < PARAREAL:
            arrived_start = passed_along(ends, "tm", 1)
            starts = jnp.where(slice_index == 0, initial_rows, arrived_start)
        previous_image = coarse_image
    ends, pressure = from_rows(jnp.stack([ends, pressure]))
    return (ends[None], pressure[None])


def solution(mesh):
    in_specs = (
        P("sx", "sy", None),
        P("sx", "sy", None),
        P("sx", "sy", None),
        P("sx", "sy", None),
        P("sx", "sy", None),
        P(),
        P(),
    )
    out_specs = (P("tm", "sx", "sy", None), P("tm", "sx", "sy", None))
    return jax.shard_map(local, mesh=mesh, in_specs=in_specs, out_specs=out_specs, check_vma=False)
```

```python
import jax
import jax.numpy as jnp
from jax import lax
from jax.sharding import PartitionSpec as P

FSTEPS = 1
NEWTON = 2
CG_ITERS = 3
SWEEPS = 3
PARAREAL = 2
ROCKS = 4


mu_water = 1.0
mu_oil = 4.0
compress = 0.05
step_dt = 0.25
damping = 0.8


def extended(array, sides, width):
    for axis, dim in sides:
        size, length = (lax.axis_size(axis), array.shape[dim])
        up = [(i, (i + 1) % size) for i in range(size - 1)]
        down = [(j, i) for i, j in up]
        last = lax.slice_in_dim(array, length - width, length, axis=dim)
        initial = lax.slice_in_dim(array, 0, width, axis=dim)
        before = lax.ppermute(last, axis, up)
        after = lax.ppermute(initial, axis, down)
        array = jnp.concatenate([before, array, after], axis=dim)
    return array


def passed_along(value, axis, steps):
    count = lax.axis_size(axis)
    initial, last = (max(0, -steps), min(count, count - steps))
    return lax.ppermute(value, axis, [(source, source + steps) for source in range(initial, last)])


def lookup(rock_cells, end_values):
    summed_total = jnp.zeros(rock_cells.shape, end_values.dtype)
    for rock_kind in range(ROCKS):
        summed_total = summed_total + jnp.where(
            rock_cells == rock_kind, end_values[rock_kind], jnp.zeros((), end_values.dtype)
        )
    return summed_total


def restrict(volume):
    return volume.reshape(
        volume.shape[0] // 2, 2, volume.shape[1] // 2, 2, volume.shape[2] // 2, 2
    ).mean(axis=(1, 3, 5))


def prolong(volume):
    first, second, third = volume.shape
    spread_out = jnp.broadcast_to(
        volume[:, None, :, None, :, None], (first, 2, second, 2, third, 2)
    )
    return spread_out.reshape(2 * first, 2 * second, 2 * third)


def pair_matrix(count):
    rows = lax.broadcasted_iota(jnp.int32, (count, 2 * count), 0)
    cols = lax.broadcasted_iota(jnp.int32, (count, 2 * count), 1)
    return (cols // 2 == rows).astype(jnp.float32)


def sum_pairs_yz(volume):
    length_y, depth_z = volume.shape[-2:]
    lead = volume.shape[:-2]
    flat = volume.reshape((-1, length_y, depth_z))
    half_z = jnp.einsum("bkz,wz->bkw", flat, pair_matrix(depth_z // 2), precision=lax.Precision.HIGHEST)
    half_y = jnp.einsum("yk,bkw->byw", pair_matrix(length_y // 2), half_z, precision=lax.Precision.HIGHEST)
    return half_y.reshape(lead + (length_y // 2, depth_z // 2))


def spread_yz(volume):
    length_y, depth_z = volume.shape[-2:]
    lead = volume.shape[:-2]
    flat = volume.reshape((-1, length_y, depth_z))
    wide_z = jnp.einsum("bkz,zw->bkw", flat, pair_matrix(depth_z), precision=lax.Precision.HIGHEST)
    wide_y = jnp.einsum("ky,bkw->byw", pair_matrix(length_y), wide_z, precision=lax.Precision.HIGHEST)
    return wide_y.reshape(lead + (2 * length_y, 2 * depth_z))


def restrict_blocks(volume):
    fields, length_x, length_y, depth_z = volume.shape
    paired_x = volume.reshape(fields, length_x // 2, 2, length_y, depth_z).sum(axis=2)
    return sum_pairs_yz(paired_x) / 8.0


def prolong_blocks(volume):
    fields, length_x, length_y, depth_z = volume.shape
    spread = spread_yz(volume)
    spread = jnp.broadcast_to(spread[:, :, None], (fields, length_x, 2) + spread.shape[2:])
    return spread.reshape((fields, 2 * length_x) + spread.shape[3:])


def pad_depth(volume):
    return jnp.pad(volume, ((0, 0), (0, 0), (1, 1)))


def face_list(padded):
    return [
        padded[2:, 1:-1, 1:-1],
        padded[:-2, 1:-1, 1:-1],
        padded[1:-1, 2:, 1:-1],
        padded[1:-1, :-2, 1:-1],
        padded[1:-1, 1:-1, 2:],
        padded[1:-1, 1:-1, :-2],
    ]


ROW_AXES = ("sx", "sy")


def row_halo(volume):
    count = lax.axis_size("sx") * lax.axis_size("sy")
    up = [(i, i + 1) for i in range(count - 1)]
    down = [(i + 1, i) for i in range(count - 1)]
    before = lax.ppermute(volume[-1:], ROW_AXES, up)
    after = lax.ppermute(volume[:1], ROW_AXES, down)
    return jnp.concatenate([before, volume, after], axis=0)


def row_faces(volume):
    return face_list(jnp.pad(row_halo(volume), ((0, 0), (1, 1), (1, 1))))


def face_mobility_values(volume):
    return row_faces(volume)


def direction_spread(volume):
    return extended(volume, (("sx", 0), ("sy", 1)), 1)


def pressure_faces(volume):
    return row_faces(volume)


def flow_faces(volume):
    return row_faces(volume)


def build_face_tables(volume):
    return face_list(pad_depth(extended(volume, (("sx", 0), ("sy", 1)), 1)))


def coarse_faces(volume):
    return face_list(pad_depth(extended(volume, (("sx", 0), ("sy", 1)), 1)))


def accumulate_terms(summand_terms):
    summed_total = summand_terms[0]
    for summand_term in summand_terms[1:]:
        summed_total = summed_total + summand_term
    return summed_total


def mobilities(saturation, water_end, oil_end):
    water_mobility = water_end * saturation * saturation / mu_water
    oil_mobility = oil_end * (1.0 - saturation) * (1.0 - saturation) / mu_oil
    return (water_mobility, oil_mobility)


def fractional(saturation, water_end, oil_end):
    water_mobility, oil_mobility = mobilities(saturation, water_end, oil_end)
    mobility = water_mobility + oil_mobility
    water_slope = 2.0 * water_end * saturation / mu_water
    oil_slope = -2.0 * oil_end * (1.0 - saturation) / mu_oil
    return (
        water_mobility / mobility,
        (water_slope * oil_mobility - water_mobility * oil_slope) / (mobility * mobility),
    )


def upwind(frac, frac_beyond, outflows):
    return accumulate_terms(
        [
            jnp.maximum(outward, 0.0) * frac + jnp.minimum(outward, 0.0) * exceeding_part
            for outward, exceeding_part in zip(outflows, frac_beyond)
        ]
    )


def global_sums(values):
    count = lax.axis_size("sx") * lax.axis_size("sy")
    packed = jnp.broadcast_to(jnp.stack(values)[None], (count, len(values)))
    gathered = lax.all_to_all(packed, ("sx", "sy"), 0, 0, tiled=True)
    totals = jnp.sum(gathered, axis=0)
    return [totals[k] for k in range(len(values))]


def extended_faces(extended):
    return face_list(jnp.pad(extended, ((0, 0), (1, 1), (1, 1))))


def apply_operator(diagonal, transmissibility, vector):
    vector_rows = row_halo(vector)
    image = diagonal * vector - accumulate_terms(
        [
            conduct_face * exceeding_part
            for conduct_face, exceeding_part in zip(transmissibility, extended_faces(vector_rows))
        ]
    )
    return image, vector_rows


def solve_pressure(source_rate, diagonal, transmissibility):
    residual = source_rate
    solution = None
    for sweep_no in range(CG_ITERS):
        precond = residual / diagonal
        image, precond_rows = apply_operator(diagonal, transmissibility, precond)
        rho_next, curvature = global_sums([jnp.sum(residual * precond), jnp.sum(precond * image)])
        if sweep_no == 0:
            step_len = rho_next / curvature
            direction = precond_rows
            applied = image
            solution = step_len * direction
        else:
            ratio = rho_next / rho_now
            step_len = rho_next / (curvature - ratio * rho_next / step_len)
            direction = precond_rows + ratio * direction
            applied = image + ratio * applied
            solution = solution + step_len * direction
        if sweep_no + 1 < CG_ITERS:
            residual = residual - step_len * applied
        rho_now = rho_next
    return solution


def fine_step(sat_old, permeability, porosity, source_rate, water_end, oil_end, beside_fields):
    permeability_rows, water_rows, oil_rows, present_rows = beside_fields
    sat_rows = row_halo(sat_old)
    water_mobility, oil_mobility = mobilities(sat_rows, water_rows, oil_rows)
    transport_rows = permeability_rows * (water_mobility + oil_mobility)
    transport_field = transport_rows[1:-1]
    transmissibility = [
        0.5 * (transport_field + exceeding_part)
        for exceeding_part in extended_faces(transport_rows)
    ]
    diagonal = compress + accumulate_terms(transmissibility)
    pressure_rows = solve_pressure(source_rate, diagonal, transmissibility)
    pressure = pressure_rows[1:-1]
    beside = extended_faces(pressure_rows)
    outflows = [
        conduct_face * (pressure - exceeding_part)
        for conduct_face, exceeding_part in zip(transmissibility, beside)
    ]
    outgoing = accumulate_terms([jnp.maximum(outward, 0.0) for outward in outflows])
    saturation = sat_old
    for newton_no in range(NEWTON):
        frac, frac_slope = fractional(saturation, water_end, oil_end)
        if newton_no == 0:
            frac_rows = jnp.where(present_rows, fractional(sat_rows, water_rows, oil_rows)[0], 0.0)
            frac_beyond = extended_faces(frac_rows)
        else:
            frac_beyond = flow_faces(frac)
        flux_sum = upwind(frac, frac_beyond, outflows)
        balance = (
            porosity * (saturation - sat_old) / step_dt
            + flux_sum
            - jnp.maximum(source_rate, 0.0)
            - jnp.minimum(source_rate, 0.0) * frac
        )
        slope_sum = porosity / step_dt + jnp.abs(frac_slope) * (
            outgoing + jnp.maximum(-source_rate, 0.0)
        )
        saturation = saturation - balance / slope_sum
    return (saturation, pressure)


def gather_grid(blocks):
    rows, cols = (lax.axis_size("sx"), lax.axis_size("sy"))
    packed = jnp.broadcast_to(blocks[None], (rows * cols,) + blocks.shape)
    gathered = lax.all_to_all(packed, ("sx", "sy"), 0, 0, tiled=True)
    fields, depth_x, depth_y, depth_z = blocks.shape
    gathered = gathered.reshape(rows, cols, fields, depth_x, depth_y, depth_z)
    gathered = gathered.transpose(2, 0, 3, 1, 4, 5)
    return gathered.reshape(fields, rows * depth_x, cols * depth_y, depth_z)


def own_block(whole, shape):
    corner = (lax.axis_index("sx") * shape[0], lax.axis_index("sy") * shape[1], 0)
    return lax.dynamic_slice(whole, corner, shape)


def to_rows(blocks):
    columns = lax.axis_size("sy")
    fields, depth_x, depth_y, depth_z = blocks.shape
    share = depth_x // columns
    packed = blocks.reshape(fields, columns, share, depth_y, depth_z).transpose(1, 0, 2, 3, 4)
    got = lax.all_to_all(packed, "sy", 0, 0, tiled=True)
    return got.transpose(1, 2, 0, 3, 4).reshape(fields, share, columns * depth_y, depth_z)


def from_rows(rows):
    columns = lax.axis_size("sy")
    fields, share, length_y, depth_z = rows.shape
    depth_y = length_y // columns
    packed = rows.reshape(fields, share, columns, depth_y, depth_z).transpose(2, 0, 1, 3, 4)
    got = lax.all_to_all(packed, "sy", 0, 0, tiled=True)
    return got.transpose(1, 0, 2, 3, 4).reshape(fields, columns * share, depth_y, depth_z)


def row_index():
    return lax.axis_index("sx") * lax.axis_size("sy") + lax.axis_index("sy")


def restrict_rows(rows):
    share, length_y, depth_z = rows.shape
    partial = sum_pairs_yz(rows)
    count = lax.axis_size("sx") * lax.axis_size("sy")
    packed = jnp.broadcast_to(partial[None], (count,) + partial.shape)
    gathered = lax.all_to_all(packed, ROW_AXES, 0, 0, tiled=True)
    gathered = gathered.reshape(count * share // 2, 2, length_y // 2, depth_z // 2)
    return gathered.sum(axis=1) / 8.0


def prolong_rows(whole, share):
    coarse_rows = (row_index() * share + jnp.arange(share)) // 2
    return spread_yz(jnp.take(whole, coarse_rows, axis=0))


def whole_faces(volume):
    return face_list(jnp.pad(volume, 1))


def local(
    initial_saturation, permeability, porosity, source_rate, rock_type, water_endpoint, oil_endpoint
):
    slices = lax.axis_size("tm")
    slice_index = lax.axis_index("tm")
    water_block = lookup(rock_type, water_endpoint)
    oil_block = lookup(rock_type, oil_endpoint)
    restricted = restrict_blocks(jnp.stack([initial_saturation, permeability, porosity, source_rate]))
    whole = gather_grid(jnp.concatenate([restricted, jnp.stack([water_block, oil_block])]))
    start_coarse, permeability_upscaled, poro_coarse, source_coarse, water_coarse, oil_coarse = (
        whole[k] for k in range(6)
    )
    water_mobility, oil_mobility = mobilities(start_coarse, water_coarse, oil_coarse)
    transport_field_upscaled = permeability_upscaled * (water_mobility + oil_mobility)
    transmissibility_upscaled = [
        (transport_field_upscaled + exceeding_part) / 8.0
        for exceeding_part in whole_faces(transport_field_upscaled)
    ]
    diag_coarse = compress + accumulate_terms(transmissibility_upscaled)
    pressure_coarse = damping * source_coarse / diag_coarse
    for sweep_no in range(SWEEPS - 1):
        coupled = accumulate_terms(
            [
                conduct_face * exceeding_part
                for conduct_face, exceeding_part in zip(
                    transmissibility_upscaled, whole_faces(pressure_coarse)
                )
            ]
        )
        pressure_coarse = (
            pressure_coarse
            + damping * (source_coarse - (diag_coarse * pressure_coarse - coupled)) / diag_coarse
        )
    flows_coarse = [
        conduct_face * (pressure_coarse - exceeding_part)
        for conduct_face, exceeding_part in zip(transmissibility_upscaled, whole_faces(pressure_coarse))
    ]
    outgoing_coarse = accumulate_terms([jnp.maximum(outward, 0.0) for outward in flows_coarse])
    coarse_dt = FSTEPS * step_dt

    def coarse_step(coarse_state):
        frac, frac_slope = fractional(coarse_state, water_coarse, oil_coarse)
        flux_sum = upwind(frac, whole_faces(frac), flows_coarse)
        balance = (
            flux_sum - jnp.maximum(source_coarse, 0.0) - jnp.minimum(source_coarse, 0.0) * frac
        )
        slope_sum = poro_coarse / coarse_dt + jnp.abs(frac_slope) * (
            outgoing_coarse + jnp.maximum(-source_coarse, 0.0)
        )
        return coarse_state - balance / slope_sum

    def chain(corrections):
        packed = jnp.broadcast_to(corrections[None], (slices,) + corrections.shape)
        every = lax.all_to_all(packed, "tm", 0, 0, tiled=True)

        def correction_before(turn_no):
            return jnp.where(turn_no > 0, every[jnp.maximum(turn_no - 1, 0)], 0.0)

        def corrected_step(turn_no, coarse_image):
            return coarse_step(coarse_image + correction_before(turn_no))

        coarse_image = lax.fori_loop(0, slice_index, corrected_step, start_coarse)
        coarse_state = coarse_image + correction_before(slice_index)
        return (coarse_state, coarse_step(coarse_state))

    coarse_state = lax.fori_loop(
        0, slice_index, lambda turn_no, state: coarse_step(state), start_coarse
    )
    coarse_image = coarse_step(coarse_state)
    water_fine, oil_fine = prolong_blocks(jnp.stack([water_block, oil_block]))
    initial_rows, permeability, porosity, source_rate, water_fine, oil_fine = to_rows(
        jnp.stack([initial_saturation, permeability, porosity, source_rate, water_fine, oil_fine])
    )
    share = initial_rows.shape[0]
    stacked_rows = row_halo(jnp.stack([permeability, water_fine, oil_fine]).transpose(1, 0, 2, 3))
    stacked_rows = stacked_rows.transpose(1, 0, 2, 3)
    count = lax.axis_size("sx") * lax.axis_size("sy")
    row_number = lax.broadcasted_iota(jnp.int32, (share + 2, 1, 1), 0) - 1 + row_index() * share
    present_rows = (row_number >= 0) & (row_number < count * share)
    beside_fields = (stacked_rows[0], stacked_rows[1], stacked_rows[2], present_rows)
    starts = jnp.where(slice_index == 0, initial_rows, prolong_rows(coarse_state, share))
    previous_image = coarse_image
    ends = starts
    pressure = starts
    for parareal_no in range(PARAREAL):
        saturation = starts
        saturation, fine_pressure = fine_step(
            saturation, permeability, porosity, source_rate, water_fine, oil_fine, beside_fields
        )
        pressure = fine_pressure
        corrections = restrict_rows(saturation) - previous_image
        coarse_state, coarse_image = chain(corrections)
        ends = prolong_rows(coarse_image, share) + saturation - prolong_rows(previous_image, share)
        if parareal_no + 1 < PARAREAL:
            arrived_start = passed_along(ends, "tm", 1)
            starts = jnp.where(slice_index == 0, initial_rows, arrived_start)
        previous_image = coarse_image
    ends, pressure = from_rows(jnp.stack([ends, pressure]))
    return (ends[None], pressure[None])


def solution(mesh):
    in_specs = (
        P("sx", "sy", None),
        P("sx", "sy", None),
        P("sx", "sy", None),
        P("sx", "sy", None),
        P("sx", "sy", None),
        P(),
        P(),
    )
    out_specs = (P("tm", "sx", "sy", None), P("tm", "sx", "sy", None))
    return jax.shard_map(local, mesh=mesh, in_specs=in_specs, out_specs=out_specs, check_vma=False)
```

```python
import jax
import jax.numpy as jnp
from jax import lax
from jax.sharding import PartitionSpec as P

FSTEPS = 1
NEWTON = 2
CG_ITERS = 3
SWEEPS = 3
PARAREAL = 2
ROCKS = 4


mu_water = 1.0
mu_oil = 4.0
compress = 0.05
step_dt = 0.25
damping = 0.8


def extended(array, sides, width):
    for axis, dim in sides:
        size, length = (lax.axis_size(axis), array.shape[dim])
        up = [(i, (i + 1) % size) for i in range(size - 1)]
        down = [(j, i) for i, j in up]
        last = lax.slice_in_dim(array, length - width, length, axis=dim)
        initial = lax.slice_in_dim(array, 0, width, axis=dim)
        before = lax.ppermute(last, axis, up)
        after = lax.ppermute(initial, axis, down)
        array = jnp.concatenate([before, array, after], axis=dim)
    return array


def passed_along(value, axis, steps):
    count = lax.axis_size(axis)
    initial, last = (max(0, -steps), min(count, count - steps))
    return lax.ppermute(value, axis, [(source, source + steps) for source in range(initial, last)])


def lookup(rock_cells, end_values):
    summed_total = jnp.zeros(rock_cells.shape, end_values.dtype)
    for rock_kind in range(ROCKS):
        summed_total = summed_total + jnp.where(
            rock_cells == rock_kind, end_values[rock_kind], jnp.zeros((), end_values.dtype)
        )
    return summed_total


def restrict(volume):
    return volume.reshape(
        volume.shape[0] // 2, 2, volume.shape[1] // 2, 2, volume.shape[2] // 2, 2
    ).mean(axis=(1, 3, 5))


def prolong(volume):
    first, second, third = volume.shape
    spread_out = jnp.broadcast_to(
        volume[:, None, :, None, :, None], (first, 2, second, 2, third, 2)
    )
    return spread_out.reshape(2 * first, 2 * second, 2 * third)


def pair_matrix(count):
    rows = lax.broadcasted_iota(jnp.int32, (count, 2 * count), 0)
    cols = lax.broadcasted_iota(jnp.int32, (count, 2 * count), 1)
    return (cols // 2 == rows).astype(jnp.float32)


def sum_pairs_yz(volume):
    length_y, depth_z = volume.shape[-2:]
    lead = volume.shape[:-2]
    flat = volume.reshape((-1, length_y, depth_z))
    half_z = jnp.einsum("bkz,wz->bkw", flat, pair_matrix(depth_z // 2), precision=lax.Precision.HIGHEST)
    half_y = jnp.einsum("yk,bkw->byw", pair_matrix(length_y // 2), half_z, precision=lax.Precision.HIGHEST)
    return half_y.reshape(lead + (length_y // 2, depth_z // 2))


def spread_yz(volume):
    length_y, depth_z = volume.shape[-2:]
    lead = volume.shape[:-2]
    flat = volume.reshape((-1, length_y, depth_z))
    wide_z = jnp.einsum("bkz,zw->bkw", flat, pair_matrix(depth_z), precision=lax.Precision.HIGHEST)
    wide_y = jnp.einsum("ky,bkw->byw", pair_matrix(length_y), wide_z, precision=lax.Precision.HIGHEST)
    return wide_y.reshape(lead + (2 * length_y, 2 * depth_z))


def restrict_blocks(volume):
    fields, length_x, length_y, depth_z = volume.shape
    paired_x = volume.reshape(fields, length_x // 2, 2, length_y, depth_z).sum(axis=2)
    return sum_pairs_yz(paired_x) / 8.0


def prolong_blocks(volume):
    fields, length_x, length_y, depth_z = volume.shape
    spread = spread_yz(volume)
    spread = jnp.broadcast_to(spread[:, :, None], (fields, length_x, 2) + spread.shape[2:])
    return spread.reshape((fields, 2 * length_x) + spread.shape[3:])


def pad_depth(volume):
    return jnp.pad(volume, ((0, 0), (0, 0), (1, 1)))


def face_list(padded):
    return [
        padded[2:, 1:-1, 1:-1],
        padded[:-2, 1:-1, 1:-1],
        padded[1:-1, 2:, 1:-1],
        padded[1:-1, :-2, 1:-1],
        padded[1:-1, 1:-1, 2:],
        padded[1:-1, 1:-1, :-2],
    ]


ROW_AXES = ("sx", "sy")


def row_halo(volume):
    count = lax.axis_size("sx") * lax.axis_size("sy")
    up = [(i, i + 1) for i in range(count - 1)]
    down = [(i + 1, i) for i in range(count - 1)]
    before = lax.ppermute(volume[-1:], ROW_AXES, up)
    after = lax.ppermute(volume[:1], ROW_AXES, down)
    return jnp.concatenate([before, volume, after], axis=0)


def row_faces(volume):
    return face_list(jnp.pad(row_halo(volume), ((0, 0), (1, 1), (1, 1))))


def face_mobility_values(volume):
    return row_faces(volume)


def direction_spread(volume):
    return extended(volume, (("sx", 0), ("sy", 1)), 1)


def pressure_faces(volume):
    return row_faces(volume)


def flow_faces(volume):
    return row_faces(volume)


def build_face_tables(volume):
    return face_list(pad_depth(extended(volume, (("sx", 0), ("sy", 1)), 1)))


def coarse_faces(volume):
    return face_list(pad_depth(extended(volume, (("sx", 0), ("sy", 1)), 1)))


def accumulate_terms(summand_terms):
    summed_total = summand_terms[0]
    for summand_term in summand_terms[1:]:
        summed_total = summed_total + summand_term
    return summed_total


def mobilities(saturation, water_end, oil_end):
    water_mobility = water_end * saturation * saturation / mu_water
    oil_mobility = oil_end * (1.0 - saturation) * (1.0 - saturation) / mu_oil
    return (water_mobility, oil_mobility)


def fractional(saturation, water_end, oil_end):
    water_mobility, oil_mobility = mobilities(saturation, water_end, oil_end)
    mobility = water_mobility + oil_mobility
    water_slope = 2.0 * water_end * saturation / mu_water
    oil_slope = -2.0 * oil_end * (1.0 - saturation) / mu_oil
    return (
        water_mobility / mobility,
        (water_slope * oil_mobility - water_mobility * oil_slope) / (mobility * mobility),
    )


def upwind(frac, frac_beyond, outflows):
    return accumulate_terms(
        [
            jnp.maximum(outward, 0.0) * frac + jnp.minimum(outward, 0.0) * exceeding_part
            for outward, exceeding_part in zip(outflows, frac_beyond)
        ]
    )


def global_sums(values):
    count = lax.axis_size("sx") * lax.axis_size("sy")
    packed = jnp.broadcast_to(jnp.stack(values)[None], (count, len(values)))
    gathered = lax.all_to_all(packed, ("sx", "sy"), 0, 0, tiled=True)
    totals = jnp.sum(gathered, axis=0)
    return [totals[k] for k in range(len(values))]


def extended_faces(extended):
    return face_list(jnp.pad(extended, ((0, 0), (1, 1), (1, 1))))


def apply_operator(diagonal, transmissibility, vector):
    vector_rows = row_halo(vector)
    image = diagonal * vector - accumulate_terms(
        [
            conduct_face * exceeding_part
            for conduct_face, exceeding_part in zip(transmissibility, extended_faces(vector_rows))
        ]
    )
    return image, vector_rows


def solve_pressure(source_rate, diagonal, transmissibility):
    residual = source_rate
    solution = None
    for sweep_no in range(CG_ITERS):
        precond = residual / diagonal
        image, precond_rows = apply_operator(diagonal, transmissibility, precond)
        rho_next, curvature = global_sums([jnp.sum(residual * precond), jnp.sum(precond * image)])
        if sweep_no == 0:
            step_len = rho_next / curvature
            direction = precond_rows
            applied = image
            solution = step_len * direction
        else:
            ratio = rho_next / rho_now
            step_len = rho_next / (curvature - ratio * rho_next / step_len)
            direction = precond_rows + ratio * direction
            applied = image + ratio * applied
            solution = solution + step_len * direction
        if sweep_no + 1 < CG_ITERS:
            residual = residual - step_len * applied
        rho_now = rho_next
    return solution


def fine_step(sat_old, permeability, porosity, source_rate, water_end, oil_end, beside_fields):
    permeability_rows, water_rows, oil_rows, present_rows = beside_fields
    sat_rows = row_halo(sat_old)
    water_mobility, oil_mobility = mobilities(sat_rows, water_rows, oil_rows)
    transport_rows = permeability_rows * (water_mobility + oil_mobility)
    transport_field = transport_rows[1:-1]
    transmissibility = [
        0.5 * (transport_field + exceeding_part)
        for exceeding_part in extended_faces(transport_rows)
    ]
    diagonal = compress + accumulate_terms(transmissibility)
    pressure_rows = solve_pressure(source_rate, diagonal, transmissibility)
    pressure = pressure_rows[1:-1]
    beside = extended_faces(pressure_rows)
    outflows = [
        conduct_face * (pressure - exceeding_part)
        for conduct_face, exceeding_part in zip(transmissibility, beside)
    ]
    outgoing = accumulate_terms([jnp.maximum(outward, 0.0) for outward in outflows])
    saturation = sat_old
    for newton_no in range(NEWTON):
        frac, frac_slope = fractional(saturation, water_end, oil_end)
        if newton_no == 0:
            frac_rows = jnp.where(present_rows, fractional(sat_rows, water_rows, oil_rows)[0], 0.0)
            frac_beyond = extended_faces(frac_rows)
        else:
            frac_beyond = flow_faces(frac)
        flux_sum = upwind(frac, frac_beyond, outflows)
        balance = (
            porosity * (saturation - sat_old) / step_dt
            + flux_sum
            - jnp.maximum(source_rate, 0.0)
            - jnp.minimum(source_rate, 0.0) * frac
        )
        slope_sum = porosity / step_dt + jnp.abs(frac_slope) * (
            outgoing + jnp.maximum(-source_rate, 0.0)
        )
        saturation = saturation - balance / slope_sum
    return (saturation, pressure)


def gather_grid(blocks):
    rows, cols = (lax.axis_size("sx"), lax.axis_size("sy"))
    packed = jnp.broadcast_to(blocks[None], (rows * cols,) + blocks.shape)
    gathered = lax.all_to_all(packed, ("sx", "sy"), 0, 0, tiled=True)
    fields, depth_x, depth_y, depth_z = blocks.shape
    gathered = gathered.reshape(rows, cols, fields, depth_x, depth_y, depth_z)
    gathered = gathered.transpose(2, 0, 3, 1, 4, 5)
    return gathered.reshape(fields, rows * depth_x, cols * depth_y, depth_z)


def own_block(whole, shape):
    corner = (lax.axis_index("sx") * shape[0], lax.axis_index("sy") * shape[1], 0)
    return lax.dynamic_slice(whole, corner, shape)


def to_rows(blocks):
    columns = lax.axis_size("sy")
    fields, depth_x, depth_y, depth_z = blocks.shape
    share = depth_x // columns
    packed = blocks.reshape(fields, columns, share, depth_y, depth_z).transpose(1, 0, 2, 3, 4)
    got = lax.all_to_all(packed, "sy", 0, 0, tiled=True)
    return got.transpose(1, 2, 0, 3, 4).reshape(fields, share, columns * depth_y, depth_z)


def from_rows(rows):
    columns = lax.axis_size("sy")
    fields, share, length_y, depth_z = rows.shape
    depth_y = length_y // columns
    packed = rows.reshape(fields, share, columns, depth_y, depth_z).transpose(2, 0, 1, 3, 4)
    got = lax.all_to_all(packed, "sy", 0, 0, tiled=True)
    return got.transpose(1, 0, 2, 3, 4).reshape(fields, columns * share, depth_y, depth_z)


def row_index():
    return lax.axis_index("sx") * lax.axis_size("sy") + lax.axis_index("sy")


def restrict_rows(rows):
    share, length_y, depth_z = rows.shape
    partial = sum_pairs_yz(rows)
    count = lax.axis_size("sx") * lax.axis_size("sy")
    packed = jnp.broadcast_to(partial[None], (count,) + partial.shape)
    gathered = lax.all_to_all(packed, ROW_AXES, 0, 0, tiled=True)
    gathered = gathered.reshape(count * share // 2, 2, length_y // 2, depth_z // 2)
    return gathered.sum(axis=1) / 8.0


def prolong_rows(whole, share):
    coarse_rows = (row_index() * share + jnp.arange(share)) // 2
    return spread_yz(jnp.take(whole, coarse_rows, axis=0))


def whole_faces(volume):
    return face_list(jnp.pad(volume, 1))


def local(
    initial_saturation, permeability, porosity, source_rate, rock_type, water_endpoint, oil_endpoint
):
    slices = lax.axis_size("tm")
    slice_index = lax.axis_index("tm")
    water_block = lookup(rock_type, water_endpoint)
    oil_block = lookup(rock_type, oil_endpoint)
    restricted = restrict_blocks(jnp.stack([initial_saturation, permeability, porosity, source_rate]))
    water_mobility, oil_mobility = mobilities(restricted[0], water_block, oil_block)
    transport_block = restricted[1] * (water_mobility + oil_mobility)
    whole = gather_grid(
        jnp.stack(
            [restricted[0], transport_block, restricted[2], restricted[3], rock_type.astype(jnp.float32)]
        )
    )
    start_coarse, transport_field_upscaled, poro_coarse, source_coarse, rock_coarse = (
        whole[k] for k in range(5)
    )
    water_coarse = lookup(rock_coarse, water_endpoint)
    oil_coarse = lookup(rock_coarse, oil_endpoint)
    transmissibility_upscaled = [
        (transport_field_upscaled + exceeding_part) / 8.0
        for exceeding_part in whole_faces(transport_field_upscaled)
    ]
    diag_coarse = compress + accumulate_terms(transmissibility_upscaled)
    pressure_coarse = damping * source_coarse / diag_coarse
    for sweep_no in range(SWEEPS - 1):
        coupled = accumulate_terms(
            [
                conduct_face * exceeding_part
                for conduct_face, exceeding_part in zip(
                    transmissibility_upscaled, whole_faces(pressure_coarse)
                )
            ]
        )
        pressure_coarse = (
            pressure_coarse
            + damping * (source_coarse - (diag_coarse * pressure_coarse - coupled)) / diag_coarse
        )
    flows_coarse = [
        conduct_face * (pressure_coarse - exceeding_part)
        for conduct_face, exceeding_part in zip(transmissibility_upscaled, whole_faces(pressure_coarse))
    ]
    outgoing_coarse = accumulate_terms([jnp.maximum(outward, 0.0) for outward in flows_coarse])
    coarse_dt = FSTEPS * step_dt

    def coarse_step(coarse_state):
        frac, frac_slope = fractional(coarse_state, water_coarse, oil_coarse)
        flux_sum = upwind(frac, whole_faces(frac), flows_coarse)
        balance = (
            flux_sum - jnp.maximum(source_coarse, 0.0) - jnp.minimum(source_coarse, 0.0) * frac
        )
        slope_sum = poro_coarse / coarse_dt + jnp.abs(frac_slope) * (
            outgoing_coarse + jnp.maximum(-source_coarse, 0.0)
        )
        return coarse_state - balance / slope_sum

    def chain(corrections):
        packed = jnp.broadcast_to(corrections[None], (slices,) + corrections.shape)
        every = lax.all_to_all(packed, "tm", 0, 0, tiled=True)

        def corrected_step(turn_no, coarse_state):
            return coarse_step(coarse_state) + every[turn_no]

        coarse_state = lax.fori_loop(0, slice_index, corrected_step, start_coarse)
        return (coarse_state, coarse_step(coarse_state))

    coarse_state = lax.fori_loop(
        0, slice_index, lambda turn_no, state: coarse_step(state), start_coarse
    )
    coarse_image = coarse_step(coarse_state)
    water_fine, oil_fine = prolong_blocks(jnp.stack([water_block, oil_block]))
    initial_rows, permeability, porosity, source_rate, water_fine, oil_fine = to_rows(
        jnp.stack([initial_saturation, permeability, porosity, source_rate, water_fine, oil_fine])
    )
    share = initial_rows.shape[0]
    stacked_rows = row_halo(jnp.stack([permeability, water_fine, oil_fine]).transpose(1, 0, 2, 3))
    stacked_rows = stacked_rows.transpose(1, 0, 2, 3)
    count = lax.axis_size("sx") * lax.axis_size("sy")
    row_number = lax.broadcasted_iota(jnp.int32, (share + 2, 1, 1), 0) - 1 + row_index() * share
    present_rows = (row_number >= 0) & (row_number < count * share)
    beside_fields = (stacked_rows[0], stacked_rows[1], stacked_rows[2], present_rows)
    starts = jnp.where(slice_index == 0, initial_rows, prolong_rows(coarse_state, share))
    previous_image = coarse_image
    ends = starts
    pressure = starts
    for parareal_no in range(PARAREAL):
        saturation = starts
        saturation, fine_pressure = fine_step(
            saturation, permeability, porosity, source_rate, water_fine, oil_fine, beside_fields
        )
        pressure = fine_pressure
        corrections = restrict_rows(saturation) - previous_image
        coarse_state, coarse_image = chain(corrections)
        ends = prolong_rows(coarse_image, share) + saturation - prolong_rows(previous_image, share)
        if parareal_no + 1 < PARAREAL:
            arrived_start = passed_along(ends, "tm", 1)
            starts = jnp.where(slice_index == 0, initial_rows, arrived_start)
        previous_image = coarse_image
    ends, pressure = from_rows(jnp.stack([ends, pressure]))
    return (ends[None], pressure[None])


def solution(mesh):
    in_specs = (
        P("sx", "sy", None),
        P("sx", "sy", None),
        P("sx", "sy", None),
        P("sx", "sy", None),
        P("sx", "sy", None),
        P(),
        P(),
    )
    out_specs = (P("tm", "sx", "sy", None), P("tm", "sx", "sy", None))
    return jax.shard_map(local, mesh=mesh, in_specs=in_specs, out_specs=out_specs, check_vma=False)
```
